32 devices in a mesh: groups: 2 (over y), seq: 4 (over z), variant: 2 (over x), mp: 2 (over core).
Axes of the slice: x: 2, y: 2, z: 4, core: 2. Of those that a mesh axis runs over, the one named last changes fastest.
Arguments:
- queries: bfloat16 [4096, 2048], P(('groups', 'seq'), 'mp'), parts along dimension 0, may hold values from -84 to 84
- keys: bfloat16 [4096, 1024], P(('groups', 'seq'), 'mp'), parts along dimension 0, may hold values from -6 to 6
- values: bfloat16 [4096, 1024], P(('groups', 'seq'), 'mp'), parts along dimension 0, may hold values from -6 to 6
- clean_keys: bfloat16 [4096, 1024], P(('groups', 'seq', 'variant'), 'mp'), parts along dimension 0, may hold values from -6 to 6
- clean_values: bfloat16 [4096, 1024], P(('groups', 'seq', 'variant'), 'mp'), parts along dimension 0, may hold values from -6 to 6
- owner_shard: int32 [4], P(('groups', 'variant')), parts along dimension 0, may hold values from 0 to 3
- span_offset: int32 [4, 2], P(('groups', 'variant')), parts along dimension 0, may hold values from 0 to 384, as said below
- span_length: int32 [4, 2], P(('groups', 'variant')), parts along dimension 0, may hold values from 128 to 256, as said below
Outputs:
- attended: bfloat16 [2, 4096, 2048], P('variant', ('groups', 'seq'), 'mp'), parts along dimension 1
The draws below stay inside these ranges and needn't reach their ends.
There are 2 independent parts, one for each index of `groups`. The reference program is written for one: setup_inputs(seed, part) draws one part's arguments, and reference() takes and returns one part's arrays. A program takes and returns all parts, laid end to end along the dimension named above; each array names one. Nothing has to cross between parts.
Inputs may be any that keep to these rules, and one draw needn't show every extreme that they name: `span_offset`: multiples of 128; span_offset + span_length <= 512 for every span. `span_length`: multiples of 128.
All inputs are finite; a program needn't handle non-finite values.
Results may differ from the reference program's by a relative error of at most 0.011.
Values may be sent and summed in bfloat16 or wider, within the bound.
No kernel may reach another device: no remote copies, remote signals or barrier semaphores. Data moves between devices by JAX's collectives and lax.ppermute only.
A program may use at most 64 MiB of HBM per device.

```python
import jax
import jax.numpy as jnp
from jax import lax

HEADS = 16
KV_HEADS = 8
HEAD_DIM = 128
WINDOW = 1024
BLOCK = 128
SPANS = 2
TOK_DEV = 512
TOKENS = 2048
VARIANTS = 2
N_SEQ = 4


def draw_pair(key):
    base_key = jax.random.fold_in(key, 11)
    query_key, keys_key = jax.random.split(base_key)
    query_cols = HEADS * HEAD_DIM
    key_cols = KV_HEADS * HEAD_DIM
    queries = jnp.clip(jax.random.normal(query_key, (TOKENS, query_cols), jnp.float32), -6.0, 6.0)
    keys = jnp.clip(jax.random.normal(keys_key, (TOKENS, key_cols), jnp.float32), -6.0, 6.0)
    return (queries, keys)


def draw_queries(key, part):
    return draw_pair(key)[0].astype(jnp.bfloat16)


def draw_keys(key, part):
    return draw_pair(key)[1].astype(jnp.bfloat16)


def draw_spans(key):
    span_key = jax.random.fold_in(key, 23)
    length_key, offset_key = jax.random.split(span_key)
    blocks_used = jax.random.randint(length_key, (VARIANTS, SPANS), 1, 3)
    blocks_used = blocks_used.at[0, 0].set(2)
    blocks_used = blocks_used.at[VARIANTS - 1, SPANS - 1].set(1)
    room = TOK_DEV // BLOCK - blocks_used + 1
    raw_draw = jax.random.randint(offset_key, (VARIANTS, SPANS), 0, 1 << 20)
    first_block = raw_draw % room
    first_block = first_block.at[VARIANTS - 1, SPANS - 1].set(TOK_DEV // BLOCK - 1)
    return ((first_block * BLOCK).astype(jnp.int32), (blocks_used * BLOCK).astype(jnp.int32))


def draw_span_offset(key, part):
    return draw_spans(key)[0]


def draw_span_length(key, part):
    return draw_spans(key)[1]


def shard_levels(own_key, shape, shards, smallest, top_value):
    def one(dim, blocks):
        draws = jax.random.uniform(jax.random.fold_in(jax.random.fold_in(own_key, 6), dim), (blocks,), jnp.float32, smallest / len(shards), top_value / len(shards))
        return jnp.repeat(jnp.exp(draws), shape[dim] // blocks).reshape((-1,) + (1,) * (len(shape) - dim - 1))

    factor_of = one(*shards[0])
    for cut in shards[1:]:
        factor_of = factor_of * one(*cut)
    return factor_of


def scatter_about(rng, shape, width, limit, cuts=(), kind=jnp.bfloat16):
    result = jax.random.normal(rng, shape, jnp.float32) * width
    if len(cuts) > 0:
        result = shard_levels(rng, shape, cuts, -0.22, 0.18) * result
    return jnp.clip(result, min=-limit, max=limit).astype(kind)


def setup_inputs(seed: int = 0, part: int = 0) -> dict:
    arg_keys = jax.random.split(jax.random.key(seed), 9)
    own_keys = jax.random.split(jax.random.fold_in(arg_keys[8], part), 9)
    queries = draw_queries(jax.random.fold_in(jax.random.fold_in(arg_keys[8], part), 71), part)
    keys = draw_keys(jax.random.fold_in(jax.random.fold_in(arg_keys[8], part), 71), part)
    values = scatter_about(own_keys[2], (TOKENS, KV_HEADS * HEAD_DIM), 1.0, 6.0, ((0, 4), (1, 2)))
    clean_keys = scatter_about(own_keys[3], (TOKENS, KV_HEADS * HEAD_DIM), 1.0, 6.0, ((0, 8), (1, 2)))
    clean_values = scatter_about(own_keys[4], (TOKENS, KV_HEADS * HEAD_DIM), 1.0, 6.0, ((0, 8), (1, 2)))
    owner_shard = jax.random.randint(own_keys[5], (VARIANTS,), 0, N_SEQ).astype(jnp.int32)
    span_offset = draw_span_offset(jax.random.fold_in(jax.random.fold_in(arg_keys[8], part), 71), part)
    span_length = draw_span_length(jax.random.fold_in(jax.random.fold_in(arg_keys[8], part), 71), part)
    return dict(queries=queries, keys=keys, values=values, clean_keys=clean_keys, clean_values=clean_values, owner_shard=owner_shard, span_offset=span_offset, span_length=span_length)


query_scale = 168.0 ** -0.5
masked_score = -1.0e30


def splice(base_rows, clean_rows, owner_index, offsets, lengths):
    position = jnp.arange(TOKENS, dtype=jnp.int32)
    inside = jnp.zeros((TOKENS,), dtype=bool)
    for span_index in range(SPANS):
        span_start = owner_index * TOK_DEV + offsets[span_index]
        inside = inside | ((position >= span_start) & (position < span_start + lengths[span_index]))
    return jnp.where(inside[:, None], clean_rows, base_rows)


def attend_block(query_block, key_window, value_window, first_row):
    row_count = query_block.shape[0]
    grouped = query_block.astype(jnp.float32).reshape(row_count, KV_HEADS, 2, HEAD_DIM)
    key_heads = key_window.astype(jnp.float32).reshape(3 * row_count, KV_HEADS, HEAD_DIM)
    value_heads = value_window.astype(jnp.float32).reshape(3 * row_count, KV_HEADS, HEAD_DIM)
    scores = jnp.einsum("qhgd,khd->hgqk", grouped, key_heads) * query_scale
    query_pos = first_row + jnp.arange(row_count, dtype=jnp.int32)
    key_pos = first_row - 2 * row_count + jnp.arange(3 * row_count, dtype=jnp.int32)
    allowed = (key_pos[None, :] <= query_pos[:, None]) & (query_pos[:, None] - key_pos[None, :] < WINDOW) & (key_pos[None, :] >= 0)
    scores = jnp.where(allowed, scores, masked_score)
    row_max = jnp.max(scores, axis=-1, keepdims=True)
    exponent = jnp.exp(scores - row_max)
    weights = (exponent / jnp.sum(exponent, axis=-1, keepdims=True)).astype(jnp.bfloat16)
    attended = jnp.einsum("hgqk,khd->qhgd", weights.astype(jnp.float32), value_heads)
    return attended.reshape(row_count, KV_HEADS * 2 * HEAD_DIM).astype(jnp.bfloat16)


def reference(queries, keys, values, clean_keys, clean_values, owner_shard, span_offset, span_length):
    padding = jnp.zeros((2 * TOK_DEV, KV_HEADS * HEAD_DIM), jnp.bfloat16)

    def one_variant(variant_index):
        owner_index = owner_shard[variant_index]
        offsets = span_offset[variant_index]
        lengths = span_length[variant_index]
        patched_keys = splice(keys, clean_keys, owner_index, offsets, lengths)
        patched_values = splice(values, clean_values, owner_index, offsets, lengths)
        key_padded = jnp.concatenate([padding, patched_keys], axis=0)
        value_padded = jnp.concatenate([padding, patched_values], axis=0)

        def one_block(block_index):
            first_row = (block_index * TOK_DEV).astype(jnp.int32)
            query_block = lax.dynamic_slice_in_dim(queries, first_row, TOK_DEV, 0)
            key_window = lax.dynamic_slice_in_dim(key_padded, first_row, 3 * TOK_DEV, 0)
            value_window = lax.dynamic_slice_in_dim(value_padded, first_row, 3 * TOK_DEV, 0)
            return attend_block(query_block, key_window, value_window, first_row)

        blocks = lax.map(one_block, jnp.arange(N_SEQ, dtype=jnp.int32))
        return blocks.reshape(TOKENS, HEADS * HEAD_DIM)

    return lax.map(one_variant, jnp.arange(VARIANTS, dtype=jnp.int32))
```

```python
import functools

import jax
import jax.numpy as jnp
from jax import lax
from jax.experimental import pallas as pl
from jax.experimental.pallas import tpu as pltpu
from jax.sharding import PartitionSpec as P

HEAD_DIM = 128
WINDOW = 1024
QUERY_BLOCK = 128

query_scale = 168.0 ** (-0.5)
masked_score = -1e30


def shifted(shard, axis, by):
    devices = lax.axis_size(axis)
    pairs = [(i, i + by) for i in range(devices) if 0 <= i + by < devices]
    return lax.ppermute(shard, axis, pairs)


def attend_kernel(first_ref, q_ref, kf_ref, kn_ref, ko_ref, vf_ref, vn_ref, vo_ref, o_ref):
    block = pl.program_id(0)
    rows = ko_ref.shape[0]
    query_count = q_ref.shape[0]
    local_heads = ko_ref.shape[1] // HEAD_DIM
    first_row = first_ref[0]
    query_local = block * query_count + lax.broadcasted_iota(jnp.int32, (query_count, rows), 0)
    key_local = lax.broadcasted_iota(jnp.int32, (query_count, rows), 1)
    query_pos = first_row + query_local
    masks = []
    for chunk in range(3):
        key_pos = first_row - (2 - chunk) * rows + key_local
        masks.append(
            (key_pos <= query_pos) & (query_pos - key_pos < WINDOW) & (key_pos >= 0)
        )
    key_refs = (kf_ref, kn_ref, ko_ref)
    value_refs = (vf_ref, vn_ref, vo_ref)
    for head_index in range(local_heads):
        cols = slice(head_index * HEAD_DIM, (head_index + 1) * HEAD_DIM)
        keys = [ref[:, cols] for ref in key_refs]
        values = [ref[:, cols] for ref in value_refs]
        for group in range(2):
            qcols = slice((2 * head_index + group) * HEAD_DIM, (2 * head_index + group + 1) * HEAD_DIM)
            query = q_ref[:, qcols]
            scores = []
            for chunk in range(3):
                s = lax.dot_general(
                    query, keys[chunk], (((1,), (1,)), ((), ())),
                    preferred_element_type=jnp.float32,
                ) * query_scale
                scores.append(jnp.where(masks[chunk], s, masked_score))
            row_max = jnp.maximum(
                jnp.maximum(jnp.max(scores[0], axis=1, keepdims=True),
                            jnp.max(scores[1], axis=1, keepdims=True)),
                jnp.max(scores[2], axis=1, keepdims=True),
            )
            exps = [jnp.exp(s - row_max) for s in scores]
            total = (
                jnp.sum(exps[0], axis=1, keepdims=True)
                + jnp.sum(exps[1], axis=1, keepdims=True)
                + jnp.sum(exps[2], axis=1, keepdims=True)
            )
            acc = None
            for chunk in range(3):
                w = (exps[chunk] / total).astype(jnp.bfloat16)
                part = jnp.dot(w, values[chunk], preferred_element_type=jnp.float32)
                acc = part if acc is None else acc + part
            o_ref[:, qcols] = acc.astype(o_ref.dtype)


def attend(queries, key_chunks, value_chunks, first_row):
    rows, key_cols = key_chunks[2].shape
    query_rows, query_cols = queries.shape
    blocks = query_rows // QUERY_BLOCK
    kv_spec = pl.BlockSpec((rows, key_cols), lambda i, f: (0, 0))
    grid_spec = pltpu.PrefetchScalarGridSpec(
        num_scalar_prefetch=1,
        grid=(blocks,),
        in_specs=[pl.BlockSpec((QUERY_BLOCK, query_cols), lambda i, f: (i, 0))] + [kv_spec] * 6,
        out_specs=pl.BlockSpec((QUERY_BLOCK, query_cols), lambda i, f: (i, 0)),
    )
    return pl.pallas_call(
        attend_kernel,
        grid_spec=grid_spec,
        out_shape=jax.ShapeDtypeStruct((query_rows, query_cols), jnp.bfloat16),
        compiler_params=pltpu.CompilerParams(dimension_semantics=("arbitrary",)),
    )(first_row.reshape(1), queries, *key_chunks, *value_chunks)


def gather_clean(clean_pair):
    variants = lax.axis_size("variant")
    if variants != 2:
        return lax.all_gather(clean_pair, "variant", axis=1, tiled=True)
    variant_index = lax.axis_index("variant")
    other = lax.ppermute(clean_pair, "variant", [(0, 1), (1, 0)])
    first = jnp.where(variant_index == 0, clean_pair, other)
    second = jnp.where(variant_index == 0, other, clean_pair)
    return jnp.concatenate([first, second], axis=1)


def shards(queries, keys, values, clean_keys, clean_values, owner_shard, span_offset, span_length):
    row_count = keys.shape[0]
    shard_index = lax.axis_index("seq")
    first_row = (shard_index * row_count).astype(jnp.int32)
    clean_full = gather_clean(jnp.stack([clean_keys, clean_values]))
    corrupt_pair = jnp.stack([keys, values])
    position = lax.broadcasted_iota(jnp.int32, (row_count,), 0)
    owner_here = owner_shard[0] == shard_index
    inside = jnp.zeros((row_count,), bool)
    for span_index in range(span_offset.shape[1]):
        start = span_offset[0, span_index]
        inside = inside | (
            (position >= start) & (position < start + span_length[0, span_index])
        )
    inside = inside & owner_here
    patched = jnp.where(inside[None, :, None], clean_full, corrupt_pair)
    near = shifted(patched, "seq", 1)
    far = shifted(near, "seq", 1)
    result = attend(
        queries,
        (far[0], near[0], patched[0]),
        (far[1], near[1], patched[1]),
        first_row,
    )
    return result[None]


def solution(mesh):
    placed = (
        P(("groups", "seq"), "mp"),
        P(("groups", "seq"), "mp"),
        P(("groups", "seq"), "mp"),
        P(("groups", "seq", "variant"), "mp"),
        P(("groups", "seq", "variant"), "mp"),
        P(("groups", "variant")),
        P(("groups", "variant"), None),
        P(("groups", "variant"), None),
    )
    return jax.shard_map(
        shards,
        mesh=mesh,
        in_specs=placed,
        out_specs=P("variant", ("groups", "seq"), "mp"),
        check_vma=False,
    )
```

```python
import jax
import jax.numpy as jnp
from jax import lax
from jax.experimental import pallas as pl
from jax.experimental.pallas import tpu as pltpu
from jax.sharding import PartitionSpec as P

HEAD_DIM = 128
WINDOW = 1024
QUERY_BLOCK = 128

query_scale = 168.0 ** (-0.5)
masked_score = -1e30


def shifted(shard, axis, by):
    devices = lax.axis_size(axis)
    pairs = [(i, i + by) for i in range(devices) if 0 <= i + by < devices]
    return lax.ppermute(shard, axis, pairs)


def chunk_kernel(chunk, first, last, rows, query_block, group):
    blocks = rows // query_block

    def kernel(first_ref, q_ref, k_ref, v_ref, *rest):
        if first:
            m_out, l_out, acc_out = rest
        elif last:
            m_in, l_in, acc_in, o_ref = rest
        else:
            m_in, l_in, acc_in, m_out, l_out, acc_out = rest
        head = pl.program_id(0)
        first_row = first_ref[0]
        stat_cols = (m_out if first else m_in).shape[1]
        for block in range(blocks):
            r0 = block * query_block
            if chunk == 2:
                k0, k1 = 0, r0 + query_block
            elif chunk == 1:
                k0, k1 = 0, rows
            else:
                k0, k1 = r0, rows
            keys = k_ref[k0:k1, :]
            values = v_ref[k0:k1, :]
            shape = (query_block, k1 - k0)
            query_pos = first_row + r0 + lax.broadcasted_iota(jnp.int32, shape, 0)
            key_pos = first_row - (2 - chunk) * rows + k0 + lax.broadcasted_iota(jnp.int32, shape, 1)
            allowed = (key_pos <= query_pos) & (query_pos - key_pos < WINDOW) & (key_pos >= 0)
            qrows = slice(r0, r0 + query_block)
            lane = lax.broadcasted_iota(jnp.int32, (query_block, stat_cols), 1)
            if not first:
                m_block = m_in[qrows, :]
                l_block = l_in[qrows, :]
            if not last:
                m_keep = m_out[qrows, :]
                l_keep = l_out[qrows, :]
            for g in range(group):
                pick = lane == group * head + g
                cols = slice(g * HEAD_DIM, (g + 1) * HEAD_DIM)
                query = q_ref[qrows, cols]
                s = lax.dot_general(
                    query, keys, (((1,), (1,)), ((), ())),
                    preferred_element_type=jnp.float32,
                ) * query_scale
                s = jnp.where(allowed, s, masked_score)
                block_max = jnp.max(s, axis=1, keepdims=True)
                if first:
                    m_new = block_max
                else:
                    m_prev = jnp.sum(jnp.where(pick, m_block, 0.0), axis=1, keepdims=True)
                    l_prev = jnp.sum(jnp.where(pick, l_block, 0.0), axis=1, keepdims=True)
                    m_new = jnp.maximum(m_prev, block_max)
                    alpha = jnp.exp(m_prev - m_new)
                p = jnp.exp(s - m_new)
                l_part = jnp.sum(p, axis=1, keepdims=True)
                pv = jnp.dot(p.astype(jnp.bfloat16), values, preferred_element_type=jnp.float32)
                if first:
                    l_new = l_part
                    acc_new = pv
                else:
                    l_new = alpha * l_prev + l_part
                    acc_new = alpha * acc_in[qrows, cols] + pv
                if last:
                    o_ref[qrows, cols] = (acc_new / l_new).astype(o_ref.dtype)
                else:
                    acc_out[qrows, cols] = acc_new
                    m_keep = jnp.where(pick, m_new, m_keep)
                    l_keep = jnp.where(pick, l_new, l_keep)
            if not last:
                m_out[qrows, :] = m_keep
                l_out[qrows, :] = l_keep

    return kernel


def attend_chunk(chunk, queries, key_rows, value_rows, first_row, state):
    rows, key_cols = key_rows.shape
    query_cols = queries.shape[1]
    kv_heads = key_cols // HEAD_DIM
    group = query_cols // key_cols
    heads = kv_heads * group
    first = state is None
    last = chunk == 0
    kernel = chunk_kernel(chunk, first, last, rows, QUERY_BLOCK, group)
    q_spec = pl.BlockSpec((rows, group * HEAD_DIM), lambda h, f: (0, h))
    kv_spec = pl.BlockSpec((rows, HEAD_DIM), lambda h, f: (0, h))
    stat_spec = pl.BlockSpec((rows, heads), lambda h, f: (0, 0))
    state_specs = [stat_spec, stat_spec, q_spec]
    in_specs = [q_spec, kv_spec, kv_spec] + ([] if first else state_specs)
    stat_shape = jax.ShapeDtypeStruct((rows, heads), jnp.float32)
    if last:
        out_specs = q_spec
        out_shape = jax.ShapeDtypeStruct((rows, query_cols), jnp.bfloat16)
    else:
        out_specs = state_specs
        out_shape = [stat_shape, stat_shape, jax.ShapeDtypeStruct((rows, query_cols), jnp.float32)]
    keys_per_row = rows + QUERY_BLOCK // 2 if chunk != 1 else rows
    cost = pl.CostEstimate(
        flops=4 * heads * rows * keys_per_row * HEAD_DIM,
        transcendentals=heads * rows * keys_per_row,
        bytes_accessed=rows * query_cols * (2 + 4 + (0 if first else 4)) + 4 * rows * key_cols,
    )
    grid_spec = pltpu.PrefetchScalarGridSpec(
        num_scalar_prefetch=1,
        grid=(kv_heads,),
        in_specs=in_specs,
        out_specs=out_specs,
    )
    return pl.pallas_call(
        kernel,
        grid_spec=grid_spec,
        out_shape=out_shape,
        cost_estimate=cost,
        compiler_params=pltpu.CompilerParams(dimension_semantics=("arbitrary",)),
    )(first_row.reshape(1), queries, key_rows, value_rows, *([] if first else state))


def gather_clean(clean_pair):
    variants = lax.axis_size("variant")
    if variants != 2:
        return lax.all_gather(clean_pair, "variant", axis=1, tiled=True)
    variant_index = lax.axis_index("variant")
    other = lax.ppermute(clean_pair, "variant", [(0, 1), (1, 0)])
    first = jnp.where(variant_index == 0, clean_pair, other)
    second = jnp.where(variant_index == 0, other, clean_pair)
    return jnp.concatenate([first, second], axis=1)


def shards(queries, keys, values, clean_keys, clean_values, owner_shard, span_offset, span_length):
    row_count = keys.shape[0]
    shard_index = lax.axis_index("seq")
    first_row = (shard_index * row_count).astype(jnp.int32)
    clean_full = gather_clean(jnp.stack([clean_keys, clean_values]))
    corrupt_pair = jnp.stack([keys, values])
    position = lax.broadcasted_iota(jnp.int32, (row_count,), 0)
    owner_here = owner_shard[0] == shard_index
    inside = jnp.zeros((row_count,), bool)
    for span_index in range(span_offset.shape[1]):
        start = span_offset[0, span_index]
        inside = inside | (
            (position >= start) & (position < start + span_length[0, span_index])
        )
    inside = inside & owner_here
    patched = jnp.where(inside[None, :, None], clean_full, corrupt_pair)
    near = shifted(patched, "seq", 1)
    far = shifted(near, "seq", 1)
    assert WINDOW == 2 * row_count
    state = attend_chunk(2, queries, patched[0], patched[1], first_row, None)
    state = attend_chunk(1, queries, near[0], near[1], first_row, state)
    result = attend_chunk(0, queries, far[0], far[1], first_row, state)
    return result[None]


def solution(mesh):
    placed = (
        P(("groups", "seq"), "mp"),
        P(("groups", "seq"), "mp"),
        P(("groups", "seq"), "mp"),
        P(("groups", "seq", "variant"), "mp"),
        P(("groups", "seq", "variant"), "mp"),
        P(("groups", "variant")),
        P(("groups", "variant"), None),
        P(("groups", "variant"), None),
    )
    return jax.shard_map(
        shards,
        mesh=mesh,
        in_specs=placed,
        out_specs=P("variant", ("groups", "seq"), "mp"),
        check_vma=False,
    )
```

```python
import jax
import jax.numpy as jnp
from jax import lax
from jax.experimental import pallas as pl
from jax.experimental.pallas import tpu as pltpu
from jax.sharding import PartitionSpec as P


HEAD_DIM = 128
WINDOW = 1024
QUERY_BLOCK = 128

query_scale = 168.0 ** (-0.5)
log2_scale = query_scale * 1.4426950408889634
masked_score = -1e30


def shifted(shard, axis, by):
    devices = lax.axis_size(axis)
    pairs = [(i, i + by) for i in range(devices) if 0 <= i + by < devices]
    return lax.ppermute(shard, axis, pairs)


def chunk_kernel(chunk, first, last, rows, query_block, group):
    blocks = rows // query_block

    def kernel(first_ref, q_ref, k_ref, v_ref, *rest):
        if first:
            m_out, l_out, acc_out = rest
        elif last:
            m_in, l_in, acc_in, o_ref = rest
        else:
            m_in, l_in, acc_in, m_out, l_out, acc_out = rest
        head = pl.program_id(0)
        first_row = first_ref[0]
        stat_cols = (m_out if first else m_in).shape[1]
        diag_shape = (query_block, query_block)
        diag_row = lax.broadcasted_iota(jnp.int32, diag_shape, 0)
        diag_col = lax.broadcasted_iota(jnp.int32, diag_shape, 1)
        diag_allowed = diag_col <= diag_row if chunk == 2 else diag_col > diag_row
        lane = lax.broadcasted_iota(jnp.int32, (query_block, stat_cols), 1)

        def compute():
            for block in range(blocks):
                r0 = block * query_block
                if chunk == 2:
                    pieces = [(0, r0, False), (r0, r0 + query_block, True)]
                elif chunk == 1:
                    pieces = [(0, rows, False)]
                else:
                    pieces = [(r0, r0 + query_block, True), (r0 + query_block, rows, False)]
                pieces = [piece for piece in pieces if piece[1] > piece[0]]
                qrows = slice(r0, r0 + query_block)
                if not first:
                    m_block = m_in[qrows, :]
                    l_block = l_in[qrows, :]
                if not last:
                    m_keep = m_out[qrows, :]
                    l_keep = l_out[qrows, :]
                for g in range(group):
                    pick = lane == group * head + g
                    cols = slice(g * HEAD_DIM, (g + 1) * HEAD_DIM)
                    query = q_ref[qrows, cols]
                    scores = []
                    for k0, k1, masked in pieces:
                        s = lax.dot_general(
                            query, k_ref[k0:k1, :], (((1,), (1,)), ((), ())),
                            preferred_element_type=jnp.float32,
                        ) * log2_scale
                        if masked:
                            s = jnp.where(diag_allowed, s, masked_score)
                        scores.append(s)
                    block_max = scores[0].max(axis=1, keepdims=True)
                    for s in scores[1:]:
                        block_max = jnp.maximum(block_max, s.max(axis=1, keepdims=True))
                    if first:
                        m_new = block_max
                    else:
                        m_prev = jnp.sum(jnp.where(pick, m_block, 0.0), axis=1, keepdims=True)
                        l_prev = jnp.sum(jnp.where(pick, l_block, 0.0), axis=1, keepdims=True)
                        m_new = jnp.maximum(m_prev, block_max)
                        alpha = jnp.exp2(m_prev - m_new)
                    l_part = None
                    pv = None
                    for (k0, k1, masked), s in zip(pieces, scores):
                        p = jnp.exp2(s - m_new)
                        part = p.sum(axis=1, keepdims=True)
                        l_part = part if l_part is None else l_part + part
                        term = jnp.dot(p.astype(jnp.bfloat16), v_ref[k0:k1, :],
                                       preferred_element_type=jnp.float32)
                        pv = term if pv is None else pv + term
                    if first:
                        l_new = l_part
                        acc_new = pv
                    else:
                        l_new = alpha * l_prev + l_part
                        acc_new = alpha * acc_in[qrows, cols] + pv
                    if last:
                        o_ref[qrows, cols] = (acc_new / l_new).astype(o_ref.dtype)
                    else:
                        acc_out[qrows, cols] = acc_new
                        m_keep = jnp.where(pick, m_new, m_keep)
                        l_keep = jnp.where(pick, l_new, l_keep)
                if not last:
                    m_out[qrows, :] = m_keep
                    l_out[qrows, :] = l_keep

        def passthrough():
            if last:
                all_lanes = lax.broadcasted_iota(jnp.int32, (rows, stat_cols), 1)
                l_all = l_in[...]
                for g in range(group):
                    cols = slice(g * HEAD_DIM, (g + 1) * HEAD_DIM)
                    l_prev = jnp.sum(jnp.where(all_lanes == group * head + g, l_all, 0.0),
                                     axis=1, keepdims=True)
                    o_ref[:, cols] = (acc_in[:, cols] / l_prev).astype(o_ref.dtype)
            else:
                m_out[...] = m_in[...]
                l_out[...] = l_in[...]
                acc_out[...] = acc_in[...]

        if chunk == 2:
            compute()
        else:
            valid = first_row >= (2 - chunk) * rows
            pl.when(valid)(compute)
            pl.when(jnp.logical_not(valid))(passthrough)

    return kernel


def attend_chunk(chunk, queries, key_rows, value_rows, first_row, state):
    rows, key_cols = key_rows.shape
    query_cols = queries.shape[1]
    kv_heads = key_cols // HEAD_DIM
    group = query_cols // key_cols
    heads = kv_heads * group
    first = state is None
    last = chunk == 0
    kernel = chunk_kernel(chunk, first, last, rows, QUERY_BLOCK, group)
    q_spec = pl.BlockSpec((rows, group * HEAD_DIM), lambda h, f: (0, h))
    kv_spec = pl.BlockSpec((rows, HEAD_DIM), lambda h, f: (0, h))
    stat_spec = pl.BlockSpec((rows, heads), lambda h, f: (0, 0))
    state_specs = [stat_spec, stat_spec, q_spec]
    in_specs = [q_spec, kv_spec, kv_spec] + ([] if first else state_specs)
    stat_shape = jax.ShapeDtypeStruct((rows, heads), jnp.float32)
    if last:
        out_specs = q_spec
        out_shape = jax.ShapeDtypeStruct((rows, query_cols), jnp.bfloat16)
    else:
        out_specs = state_specs
        out_shape = [stat_shape, stat_shape, jax.ShapeDtypeStruct((rows, query_cols), jnp.float32)]
    keys_per_row = rows + QUERY_BLOCK // 2 if chunk != 1 else rows
    cost = pl.CostEstimate(
        flops=4 * heads * rows * keys_per_row * HEAD_DIM,
        transcendentals=heads * rows * keys_per_row,
        bytes_accessed=rows * query_cols * (2 + 4 + (0 if first else 4)) + 4 * rows * key_cols,
    )
    grid_spec = pltpu.PrefetchScalarGridSpec(
        num_scalar_prefetch=1,
        grid=(kv_heads,),
        in_specs=in_specs,
        out_specs=out_specs,
    )
    return pl.pallas_call(
        kernel,
        grid_spec=grid_spec,
        out_shape=out_shape,
        cost_estimate=cost,
        compiler_params=pltpu.CompilerParams(dimension_semantics=("arbitrary",)),
    )(first_row.reshape(1), queries, key_rows, value_rows, *([] if first else state))


def swap_variant(half):
    variants = lax.axis_size("variant")
    return lax.ppermute(half, "variant", [(i, (i + 1) % variants) for i in range(variants)])


def halves_in_order(own, other, variant_index):
    return jnp.where(
        variant_index == 0,
        jnp.concatenate([own, other], axis=1),
        jnp.concatenate([other, own], axis=1),
    )


def shard_body(queries, keys, values, clean_keys, clean_values, owner_shard, span_offset, span_length):
    row_count = keys.shape[0]
    assert WINDOW == 2 * row_count
    shard_index = lax.axis_index("seq")
    first_row = (shard_index * row_count).astype(jnp.int32)
    position = lax.broadcasted_iota(jnp.int32, (row_count,), 0)
    inside = jnp.zeros((row_count,), bool)
    for span_index in range(span_offset.shape[1]):
        start = span_offset[0, span_index]
        inside = inside | (
            (position >= start) & (position < start + span_length[0, span_index])
        )
    inside = inside & (owner_shard[0] == shard_index)
    corrupt_pair = jnp.stack([keys, values])
    clean_own = jnp.stack([clean_keys, clean_values])
    if lax.axis_size("variant") != 2:
        clean_full = lax.all_gather(clean_own, "variant", axis=1, tiled=True)
        patched = jnp.where(inside[None, :, None], clean_full, corrupt_pair)
        near = shifted(patched, "seq", 1)
        far = shifted(near, "seq", 1)
    else:
        half = row_count // 2
        variant_index = lax.axis_index("variant")
        lo, hi = corrupt_pair[:, :half], corrupt_pair[:, half:]
        inside_lo, inside_hi = inside[:half], inside[half:]
        corrupt_own = jnp.where(variant_index == 0, lo, hi)
        corrupt_other = jnp.where(variant_index == 0, hi, lo)
        inside_own = jnp.where(variant_index == 0, inside_lo, inside_hi)
        inside_other = jnp.where(variant_index == 0, inside_hi, inside_lo)
        own_half = jnp.where(inside_own[None, :, None], clean_own, corrupt_own)
        own_half, clean_own = lax.optimization_barrier((own_half, clean_own))
        near_own = shifted(own_half, "seq", 1)
        clean_other = swap_variant(clean_own)
        other_half = jnp.where(inside_other[None, :, None], clean_other, corrupt_other)
        near_other = shifted(other_half, "seq", 1)
        far_own = shifted(near_own, "seq", 1)
        far_other = shifted(near_other, "seq", 1)
        patched = halves_in_order(own_half, other_half, variant_index)
        near = halves_in_order(near_own, near_other, variant_index)
        far = halves_in_order(far_own, far_other, variant_index)
    state = attend_chunk(2, queries, patched[0], patched[1], first_row, None)
    state = attend_chunk(1, queries, near[0], near[1], first_row, state)
    result = attend_chunk(0, queries, far[0], far[1], first_row, state)
    return result[None]


def solution(mesh):
    placed = (
        P(("groups", "seq"), "mp"),
        P(("groups", "seq"), "mp"),
        P(("groups", "seq"), "mp"),
        P(("groups", "seq", "variant"), "mp"),
        P(("groups", "seq", "variant"), "mp"),
        P(("groups", "variant")),
        P(("groups", "variant"), None),
        P(("groups", "variant"), None),
    )
    return jax.shard_map(
        shard_body,
        mesh=mesh,
        in_specs=placed,
        out_specs=P("variant", ("groups", "seq"), "mp"),
        check_vma=False,
    )
```

```python
import jax
import jax.numpy as jnp
from jax import lax
from jax.experimental import pallas as pl
from jax.experimental.pallas import tpu as pltpu
from jax.sharding import PartitionSpec as P


HEAD_DIM = 128
WINDOW = 1024
QUERY_BLOCK = 128

query_scale = 168.0 ** (-0.5)
log2_scale = query_scale * 1.4426950408889634
masked_score = -1e30


def shifted(shard, axis, by):
    devices = lax.axis_size(axis)
    pairs = [(i, i + by) for i in range(devices) if 0 <= i + by < devices]
    return lax.ppermute(shard, axis, pairs)


def row_reduce(x, combine, reduce):
    lanes = 128
    partial = x[:, :lanes]
    for start in range(lanes, x.shape[1], lanes):
        partial = combine(partial, x[:, start:start + lanes])
    return reduce(partial, axis=1, keepdims=True)


def chunk_kernel(chunk, first, last, rows, key_rows, query_block, group):
    blocks = rows // query_block

    def kernel(first_ref, q_ref, k_ref, v_ref, *rest):
        if first:
            m_out, l_out, acc_out = rest
        elif last:
            m_in, l_in, acc_in, o_ref = rest
        else:
            m_in, l_in, acc_in, m_out, l_out, acc_out = rest
        head = pl.program_id(0)
        first_row = first_ref[0]
        stat_cols = (m_out if first else m_in).shape[1]
        diag_shape = (query_block, query_block)
        diag_row = lax.broadcasted_iota(jnp.int32, diag_shape, 0)
        diag_col = lax.broadcasted_iota(jnp.int32, diag_shape, 1)
        diag_allowed = diag_col <= diag_row if chunk == 2 else diag_col > diag_row
        lane = lax.broadcasted_iota(jnp.int32, (query_block, stat_cols), 1)

        def compute():
            for block in range(blocks):
                r0 = block * query_block
                if chunk == 2:
                    pieces = [(0, r0, False), (r0, r0 + query_block, True)]
                elif chunk == 1:
                    pieces = [(0, key_rows, False)]
                else:
                    pieces = [(r0, r0 + query_block, True), (r0 + query_block, rows, False)]
                pieces = [piece for piece in pieces if piece[1] > piece[0]]
                qrows = slice(r0, r0 + query_block)
                if not first:
                    m_block = m_in[qrows, :]
                    l_block = l_in[qrows, :]
                if not last:
                    m_keep = m_out[qrows, :]
                    l_keep = l_out[qrows, :]
                for g in range(group):
                    pick = lane == group * head + g
                    cols = slice(g * HEAD_DIM, (g + 1) * HEAD_DIM)
                    query = q_ref[qrows, cols]
                    scores = []
                    for k0, k1, masked in pieces:
                        s = lax.dot_general(
                            query, k_ref[k0:k1, :], (((1,), (1,)), ((), ())),
                            preferred_element_type=jnp.float32,
                        ) * log2_scale
                        if masked:
                            s = jnp.where(diag_allowed, s, masked_score)
                        scores.append(s)
                    block_max = row_reduce(jnp.concatenate(scores, axis=1) if len(scores) > 1 else scores[0],
                                           jnp.maximum, jnp.max)
                    if first:
                        m_new = block_max
                    else:
                        m_prev = jnp.sum(jnp.where(pick, m_block, 0.0), axis=1, keepdims=True)
                        l_prev = jnp.sum(jnp.where(pick, l_block, 0.0), axis=1, keepdims=True)
                        m_new = jnp.maximum(m_prev, block_max)
                        alpha = jnp.exp2(m_prev - m_new)
                    l_part = None
                    pv = None
                    for (k0, k1, masked), s in zip(pieces, scores):
                        p = jnp.exp2(s - m_new)
                        part = row_reduce(p, jnp.add, jnp.sum)
                        l_part = part if l_part is None else l_part + part
                        term = jnp.dot(p.astype(jnp.bfloat16), v_ref[k0:k1, :],
                                       preferred_element_type=jnp.float32)
                        pv = term if pv is None else pv + term
                    if first:
                        l_new = l_part
                        acc_new = pv
                    else:
                        l_new = alpha * l_prev + l_part
                        acc_new = alpha * acc_in[qrows, cols] + pv
                    if last:
                        o_ref[qrows, cols] = (acc_new / l_new).astype(o_ref.dtype)
                    else:
                        acc_out[qrows, cols] = acc_new
                        m_keep = jnp.where(pick, m_new, m_keep)
                        l_keep = jnp.where(pick, l_new, l_keep)
                if not last:
                    m_out[qrows, :] = m_keep
                    l_out[qrows, :] = l_keep

        def passthrough():
            if last:
                all_lanes = lax.broadcasted_iota(jnp.int32, (rows, stat_cols), 1)
                l_all = l_in[...]
                for g in range(group):
                    cols = slice(g * HEAD_DIM, (g + 1) * HEAD_DIM)
                    l_prev = jnp.sum(jnp.where(all_lanes == group * head + g, l_all, 0.0),
                                     axis=1, keepdims=True)
                    o_ref[:, cols] = (acc_in[:, cols] / l_prev).astype(o_ref.dtype)
            else:
                m_out[...] = m_in[...]
                l_out[...] = l_in[...]
                acc_out[...] = acc_in[...]

        if chunk == 2:
            compute()
        else:
            valid = first_row >= (2 - chunk) * rows
            pl.when(valid)(compute)
            pl.when(jnp.logical_not(valid))(passthrough)

    return kernel


def attend_chunk(chunk, queries, key_rows, value_rows, first_row, state):
    key_count, key_cols = key_rows.shape
    rows, query_cols = queries.shape
    kv_heads = key_cols // HEAD_DIM
    group = query_cols // key_cols
    heads = kv_heads * group
    first = state is None
    last = chunk == 0
    kernel = chunk_kernel(chunk, first, last, rows, key_count, QUERY_BLOCK, group)
    q_spec = pl.BlockSpec((rows, group * HEAD_DIM), lambda h, f: (0, h))
    kv_spec = pl.BlockSpec((key_count, HEAD_DIM), lambda h, f: (0, h))
    stat_spec = pl.BlockSpec((rows, heads), lambda h, f: (0, 0))
    state_specs = [stat_spec, stat_spec, q_spec]
    in_specs = [q_spec, kv_spec, kv_spec] + ([] if first else state_specs)
    stat_shape = jax.ShapeDtypeStruct((rows, heads), jnp.float32)
    if last:
        out_specs = q_spec
        out_shape = jax.ShapeDtypeStruct((rows, query_cols), jnp.bfloat16)
    else:
        out_specs = state_specs
        out_shape = [stat_shape, stat_shape, jax.ShapeDtypeStruct((rows, query_cols), jnp.float32)]
    keys_per_row = rows // 2 + QUERY_BLOCK // 2 if chunk != 1 else key_count
    cost = pl.CostEstimate(
        flops=4 * heads * rows * keys_per_row * HEAD_DIM,
        transcendentals=heads * rows * keys_per_row,
        bytes_accessed=rows * query_cols * (2 + 4 + (0 if first else 4)) + 4 * key_count * key_cols,
    )
    grid_spec = pltpu.PrefetchScalarGridSpec(
        num_scalar_prefetch=1,
        grid=(kv_heads,),
        in_specs=in_specs,
        out_specs=out_specs,
    )
    return pl.pallas_call(
        kernel,
        grid_spec=grid_spec,
        out_shape=out_shape,
        cost_estimate=cost,
        compiler_params=pltpu.CompilerParams(dimension_semantics=("arbitrary",)),
    )(first_row.reshape(1), queries, key_rows, value_rows, *([] if first else state))


def swap_variant(half):
    variants = lax.axis_size("variant")
    return lax.ppermute(half, "variant", [(i, (i + 1) % variants) for i in range(variants)])


def halves_in_order(own, other, variant_index):
    return jnp.where(
        variant_index == 0,
        jnp.concatenate([own, other], axis=1),
        jnp.concatenate([other, own], axis=1),
    )


def shard_body(queries, keys, values, clean_keys, clean_values, owner_shard, span_offset, span_length):
    row_count = keys.shape[0]
    assert WINDOW == 2 * row_count
    shard_index = lax.axis_index("seq")
    first_row = (shard_index * row_count).astype(jnp.int32)
    position = lax.broadcasted_iota(jnp.int32, (row_count,), 0)
    inside = jnp.zeros((row_count,), bool)
    for span_index in range(span_offset.shape[1]):
        start = span_offset[0, span_index]
        inside = inside | (
            (position >= start) & (position < start + span_length[0, span_index])
        )
    inside = inside & (owner_shard[0] == shard_index)
    corrupt_pair = jnp.stack([keys, values])
    clean_own = jnp.stack([clean_keys, clean_values])
    if lax.axis_size("variant") != 2:
        clean_full = lax.all_gather(clean_own, "variant", axis=1, tiled=True)
        patched = jnp.where(inside[None, :, None], clean_full, corrupt_pair)
        near = shifted(patched, "seq", 1)
        far = shifted(near, "seq", 1)
        near_parts = (near,)
    else:
        half = row_count // 2
        variant_index = lax.axis_index("variant")
        lo, hi = corrupt_pair[:, :half], corrupt_pair[:, half:]
        inside_lo, inside_hi = inside[:half], inside[half:]
        corrupt_own = jnp.where(variant_index == 0, lo, hi)
        corrupt_other = jnp.where(variant_index == 0, hi, lo)
        inside_own = jnp.where(variant_index == 0, inside_lo, inside_hi)
        inside_other = jnp.where(variant_index == 0, inside_hi, inside_lo)
        own_half = jnp.where(inside_own[None, :, None], clean_own, corrupt_own)
        own_half, clean_own = lax.optimization_barrier((own_half, clean_own))
        near_own = shifted(own_half, "seq", 1)
        clean_other = swap_variant(clean_own)
        other_half = jnp.where(inside_other[None, :, None], clean_other, corrupt_other)
        near_other = shifted(other_half, "seq", 1)
        far_own = shifted(near_own, "seq", 1)
        far_other = shifted(near_other, "seq", 1)
        patched = halves_in_order(own_half, other_half, variant_index)
        far = halves_in_order(far_own, far_other, variant_index)
        near_parts = (near_own, near_other)
    state = attend_chunk(2, queries, patched[0], patched[1], first_row, None)
    for part in near_parts:
        state = attend_chunk(1, queries, part[0], part[1], first_row, state)
    result = attend_chunk(0, queries, far[0], far[1], first_row, state)
    return result[None]


def solution(mesh):
    placed = (
        P(("groups", "seq"), "mp"),
        P(("groups", "seq"), "mp"),
        P(("groups", "seq"), "mp"),
        P(("groups", "seq", "variant"), "mp"),
        P(("groups", "seq", "variant"), "mp"),
        P(("groups", "variant")),
        P(("groups", "variant"), None),
        P(("groups", "variant"), None),
    )
    return jax.shard_map(
        shard_body,
        mesh=mesh,
        in_specs=placed,
        out_specs=P("variant", ("groups", "seq"), "mp"),
        check_vma=False,
    )
```

```python
import jax
import jax.numpy as jnp
from jax import lax
from jax.experimental import pallas as pl
from jax.experimental.pallas import tpu as pltpu
from jax.sharding import PartitionSpec as P


HEAD_DIM = 128
WINDOW = 1024
QUERY_BLOCK = 128

query_scale = 168.0 ** (-0.5)
log2_scale = query_scale * 1.4426950408889634
masked_score = -1e30


def shifted(shard, axis, by):
    devices = lax.axis_size(axis)
    pairs = [(i, i + by) for i in range(devices) if 0 <= i + by < devices]
    return lax.ppermute(shard, axis, pairs)


def row_reduce(x, combine, reduce):
    lanes = 128
    partial = x[:, :lanes]
    for start in range(lanes, x.shape[1], lanes):
        partial = combine(partial, x[:, start:start + lanes])
    return reduce(partial, axis=1, keepdims=True)


def chunk_kernel(chunk, first, last, rows, key_rows, query_block, group):
    blocks = rows // query_block

    def kernel(first_ref, q_ref, k_ref, v_ref, *rest):
        if first:
            m_out, l_out, acc_out = rest
        elif last:
            m_in, l_in, acc_in, o_ref = rest
        else:
            m_in, l_in, acc_in, m_out, l_out, acc_out = rest
        head = pl.program_id(0)
        first_row = first_ref[0]
        stat_cols = (m_out if first else m_in).shape[1]
        diag_shape = (query_block, query_block)
        diag_row = lax.broadcasted_iota(jnp.int32, diag_shape, 0)
        diag_col = lax.broadcasted_iota(jnp.int32, diag_shape, 1)
        diag_allowed = diag_col <= diag_row if chunk == 2 else diag_col > diag_row
        lane = lax.broadcasted_iota(jnp.int32, (query_block, stat_cols), 1)

        def compute():
            for block in range(blocks):
                r0 = block * query_block
                if chunk == 2:
                    pieces = [(0, r0, False), (r0, r0 + query_block, True)]
                elif chunk == 1:
                    pieces = [(0, key_rows, False)]
                else:
                    pieces = [(r0, r0 + query_block, True), (r0 + query_block, rows, False)]
                pieces = [piece for piece in pieces if piece[1] > piece[0]]
                qrows = slice(r0, r0 + query_block)
                if not first:
                    m_block = m_in[qrows, :]
                    l_block = l_in[qrows, :]
                if not last:
                    m_keep = m_out[qrows, :]
                    l_keep = l_out[qrows, :]
                for g in range(group):
                    pick = lane == group * head + g
                    cols = slice(g * HEAD_DIM, (g + 1) * HEAD_DIM)
                    query = q_ref[qrows, cols]
                    scores = []
                    for k0, k1, masked in pieces:
                        s = lax.dot_general(
                            query, k_ref[k0:k1, :], (((1,), (1,)), ((), ())),
                            preferred_element_type=jnp.float32,
                        ) * log2_scale
                        if masked:
                            s = jnp.where(diag_allowed, s, masked_score)
                        scores.append(s)
                    block_max = row_reduce(jnp.concatenate(scores, axis=1) if len(scores) > 1 else scores[0],
                                           jnp.maximum, jnp.max)
                    if first:
                        m_new = block_max
                    else:
                        m_prev = jnp.sum(jnp.where(pick, m_block, 0.0), axis=1, keepdims=True)
                        l_prev = jnp.sum(jnp.where(pick, l_block, 0.0), axis=1, keepdims=True)
                        m_new = jnp.maximum(m_prev, block_max)
                        alpha = jnp.exp2(m_prev - m_new)
                    l_part = None
                    pv = None
                    for (k0, k1, masked), s in zip(pieces, scores):
                        p = jnp.exp2(s - m_new)
                        part = row_reduce(p, jnp.add, jnp.sum)
                        l_part = part if l_part is None else l_part + part
                        term = jnp.dot(p.astype(jnp.bfloat16), v_ref[k0:k1, :],
                                       preferred_element_type=jnp.float32)
                        pv = term if pv is None else pv + term
                    if first:
                        l_new = l_part
                        acc_new = pv
                    else:
                        l_new = alpha * l_prev + l_part
                        acc_new = alpha * acc_in[qrows, cols] + pv
                    if last:
                        o_ref[qrows, cols] = (acc_new / l_new).astype(o_ref.dtype)
                    else:
                        acc_out[qrows, cols] = acc_new
                        m_keep = jnp.where(pick, m_new, m_keep)
                        l_keep = jnp.where(pick, l_new, l_keep)
                if not last:
                    m_out[qrows, :] = m_keep
                    l_out[qrows, :] = l_keep

        def passthrough():
            if last:
                all_lanes = lax.broadcasted_iota(jnp.int32, (rows, stat_cols), 1)
                l_all = l_in[...]
                for g in range(group):
                    cols = slice(g * HEAD_DIM, (g + 1) * HEAD_DIM)
                    l_prev = jnp.sum(jnp.where(all_lanes == group * head + g, l_all, 0.0),
                                     axis=1, keepdims=True)
                    o_ref[:, cols] = (acc_in[:, cols] / l_prev).astype(o_ref.dtype)
            else:
                m_out[...] = m_in[...]
                l_out[...] = l_in[...]
                acc_out[...] = acc_in[...]

        if chunk == 2:
            compute()
        else:
            valid = first_row >= (2 - chunk) * rows
            pl.when(valid)(compute)
            pl.when(jnp.logical_not(valid))(passthrough)

    return kernel


def attend_chunk(chunk, queries, key_rows, value_rows, first_row, state):
    key_count, key_cols = key_rows.shape
    rows, query_cols = queries.shape
    kv_heads = key_cols // HEAD_DIM
    group = query_cols // key_cols
    heads = kv_heads * group
    first = state is None
    last = chunk == 0
    kernel = chunk_kernel(chunk, first, last, rows, key_count, QUERY_BLOCK, group)
    q_spec = pl.BlockSpec((rows, group * HEAD_DIM), lambda h, f: (0, h))
    kv_spec = pl.BlockSpec((key_count, HEAD_DIM), lambda h, f: (0, h))
    stat_spec = pl.BlockSpec((rows, heads), lambda h, f: (0, 0))
    state_specs = [stat_spec, stat_spec, q_spec]
    in_specs = [q_spec, kv_spec, kv_spec] + ([] if first else state_specs)
    stat_shape = jax.ShapeDtypeStruct((rows, heads), jnp.float32)
    if last:
        out_specs = q_spec
        out_shape = jax.ShapeDtypeStruct((rows, query_cols), jnp.bfloat16)
    else:
        out_specs = state_specs
        out_shape = [stat_shape, stat_shape, jax.ShapeDtypeStruct((rows, query_cols), jnp.float32)]
    keys_per_row = rows // 2 + QUERY_BLOCK // 2 if chunk != 1 else key_count
    cost = pl.CostEstimate(
        flops=4 * heads * rows * keys_per_row * HEAD_DIM,
        transcendentals=heads * rows * keys_per_row,
        bytes_accessed=rows * query_cols * (2 + 4 + (0 if first else 4)) + 4 * key_count * key_cols,
    )
    grid_spec = pltpu.PrefetchScalarGridSpec(
        num_scalar_prefetch=1,
        grid=(kv_heads,),
        in_specs=in_specs,
        out_specs=out_specs,
    )
    return pl.pallas_call(
        kernel,
        grid_spec=grid_spec,
        out_shape=out_shape,
        cost_estimate=cost,
        compiler_params=pltpu.CompilerParams(dimension_semantics=("arbitrary",)),
    )(first_row.reshape(1), queries, key_rows, value_rows, *([] if first else state))


def swap_variant(half):
    variants = lax.axis_size("variant")
    return lax.ppermute(half, "variant", [(i, (i + 1) % variants) for i in range(variants)])


def halves_in_order(own, other, variant_index):
    return jnp.where(
        variant_index == 0,
        jnp.concatenate([own, other], axis=1),
        jnp.concatenate([other, own], axis=1),
    )


def shard_body(queries, keys, values, clean_keys, clean_values, owner_shard, span_offset, span_length):
    row_count = keys.shape[0]
    assert WINDOW == 2 * row_count
    shard_index = lax.axis_index("seq")
    first_row = (shard_index * row_count).astype(jnp.int32)
    position = lax.broadcasted_iota(jnp.int32, (row_count, span_offset.shape[1]), 0)
    in_span = (position >= span_offset) & (position < span_offset + span_length)
    in_span = in_span & (owner_shard[:, None] == shard_index)
    inside = jnp.any(in_span, axis=1)
    corrupt_pair = jnp.stack([keys, values])
    clean_own = jnp.stack([clean_keys, clean_values])
    if lax.axis_size("variant") != 2:
        clean_full = lax.all_gather(clean_own, "variant", axis=1, tiled=True)
        patched = jnp.where(inside[None, :, None], clean_full, corrupt_pair)
        near = shifted(patched, "seq", 1)
        far = shifted(near, "seq", 1)
        near_parts = (near,)
    else:
        half = row_count // 2
        variant_index = lax.axis_index("variant")
        lo, hi = corrupt_pair[:, :half], corrupt_pair[:, half:]
        inside_lo, inside_hi = inside[:half], inside[half:]
        corrupt_own = jnp.where(variant_index == 0, lo, hi)
        corrupt_other = jnp.where(variant_index == 0, hi, lo)
        inside_own = jnp.where(variant_index == 0, inside_lo, inside_hi)
        inside_other = jnp.where(variant_index == 0, inside_hi, inside_lo)
        own_half = jnp.where(inside_own[None, :, None], clean_own, corrupt_own)
        own_half, clean_own = lax.optimization_barrier((own_half, clean_own))
        near_own = shifted(own_half, "seq", 1)
        clean_other = swap_variant(clean_own)
        other_half = jnp.where(inside_other[None, :, None], clean_other, corrupt_other)
        near_other = shifted(other_half, "seq", 1)
        far_own = shifted(near_own, "seq", 1)
        far_other = shifted(near_other, "seq", 1)
        patched = halves_in_order(own_half, other_half, variant_index)
        far = halves_in_order(far_own, far_other, variant_index)
        near_parts = (near_own, near_other)
    state = attend_chunk(2, queries, patched[0], patched[1], first_row, None)
    for part in near_parts:
        state = attend_chunk(1, queries, part[0], part[1], first_row, state)
    result = attend_chunk(0, queries, far[0], far[1], first_row, state)
    return result[None]


def solution(mesh):
    placed = (
        P(("groups", "seq"), "mp"),
        P(("groups", "seq"), "mp"),
        P(("groups", "seq"), "mp"),
        P(("groups", "seq", "variant"), "mp"),
        P(("groups", "seq", "variant"), "mp"),
        P(("groups", "variant")),
        P(("groups", "variant"), None),
        P(("groups", "variant"), None),
    )
    return jax.shard_map(
        shard_body,
        mesh=mesh,
        in_specs=placed,
        out_specs=P("variant", ("groups", "seq"), "mp"),
        check_vma=False,
    )
```

```python
import functools

import jax
import jax.numpy as jnp
from jax import lax
from jax.experimental import pallas as pl
from jax.experimental.pallas import tpu as pltpu
from jax.sharding import PartitionSpec as P


HEAD_DIM = 128
WINDOW = 1024
QUERY_BLOCK = 128
MASKED_QUERY_BLOCK = 256

query_scale = 168.0 ** (-0.5)
log2_scale = query_scale * 1.4426950408889634
masked_score = -1e30


def shifted(shard, axis, by):
    devices = lax.axis_size(axis)
    pairs = [(i, i + by) for i in range(devices) if 0 <= i + by < devices]
    return lax.ppermute(shard, axis, pairs)


def row_reduce(x, combine, reduce):
    lanes = 128
    partial = x[:, :lanes]
    for start in range(lanes, x.shape[1], lanes):
        partial = combine(partial, x[:, start:start + lanes])
    return reduce(partial, axis=1, keepdims=True)


def chunk_kernel(chunk, first, last, rows, key_rows, query_block, group):
    blocks = rows // query_block

    def kernel(first_ref, q_ref, k_ref, v_ref, *rest):
        if first:
            m_out, l_out, acc_out = rest
        elif last:
            m_in, l_in, acc_in, o_ref = rest
        else:
            m_in, l_in, acc_in, m_out, l_out, acc_out = rest
        head = pl.program_id(0)
        first_row = first_ref[0]
        stat_cols = (m_out if first else m_in).shape[1]
        diag_shape = (query_block, query_block)
        diag_row = lax.broadcasted_iota(jnp.int32, diag_shape, 0)
        diag_col = lax.broadcasted_iota(jnp.int32, diag_shape, 1)
        diag_allowed = diag_col <= diag_row if chunk == 2 else diag_col > diag_row
        lane = lax.broadcasted_iota(jnp.int32, (query_block, stat_cols), 1)

        def compute():
            for block in range(blocks):
                r0 = block * query_block
                if chunk == 2:
                    pieces = [(0, r0, False), (r0, r0 + query_block, True)]
                elif chunk == 1:
                    pieces = [(0, key_rows, False)]
                else:
                    pieces = [(r0, r0 + query_block, True), (r0 + query_block, rows, False)]
                pieces = [piece for piece in pieces if piece[1] > piece[0]]
                qrows = slice(r0, r0 + query_block)
                if not first:
                    m_block = m_in[qrows, :]
                    l_block = l_in[qrows, :]
                if not last:
                    m_keep = m_out[qrows, :]
                    l_keep = l_out[qrows, :]
                for g in range(group):
                    pick = lane == group * head + g
                    cols = slice(g * HEAD_DIM, (g + 1) * HEAD_DIM)
                    query = q_ref[qrows, cols]
                    scores = []
                    for k0, k1, masked in pieces:
                        s = lax.dot_general(
                            query, k_ref[k0:k1, :], (((1,), (1,)), ((), ())),
                            preferred_element_type=jnp.float32,
                        ) * log2_scale
                        if masked:
                            s = jnp.where(diag_allowed, s, masked_score)
                        scores.append(s)
                    block_max = row_reduce(jnp.concatenate(scores, axis=1) if len(scores) > 1 else scores[0],
                                           jnp.maximum, jnp.max)
                    if first:
                        m_new = block_max
                    else:
                        m_prev = jnp.sum(jnp.where(pick, m_block, 0.0), axis=1, keepdims=True)
                        l_prev = jnp.sum(jnp.where(pick, l_block, 0.0), axis=1, keepdims=True)
                        m_new = jnp.maximum(m_prev, block_max)
                        alpha = jnp.exp2(m_prev - m_new)
                    l_part = None
                    pv = None
                    for (k0, k1, masked), s in zip(pieces, scores):
                        p = jnp.exp2(s - m_new)
                        part = row_reduce(p, jnp.add, jnp.sum)
                        l_part = part if l_part is None else l_part + part
                        term = jnp.dot(p.astype(jnp.bfloat16), v_ref[k0:k1, :],
                                       preferred_element_type=jnp.float32)
                        pv = term if pv is None else pv + term
                    if first:
                        l_new = l_part
                        acc_new = pv
                    else:
                        l_new = alpha * l_prev + l_part
                        acc_new = alpha * acc_in[qrows, cols] + pv
                    if last:
                        o_ref[qrows, cols] = (acc_new / l_new).astype(o_ref.dtype)
                    else:
                        acc_out[qrows, cols] = acc_new
                        m_keep = jnp.where(pick, m_new, m_keep)
                        l_keep = jnp.where(pick, l_new, l_keep)
                if not last:
                    m_out[qrows, :] = m_keep
                    l_out[qrows, :] = l_keep

        def passthrough():
            if last:
                all_lanes = lax.broadcasted_iota(jnp.int32, (rows, stat_cols), 1)
                l_all = l_in[...]
                for g in range(group):
                    cols = slice(g * HEAD_DIM, (g + 1) * HEAD_DIM)
                    l_prev = jnp.sum(jnp.where(all_lanes == group * head + g, l_all, 0.0),
                                     axis=1, keepdims=True)
                    o_ref[:, cols] = (acc_in[:, cols] / l_prev).astype(o_ref.dtype)
            else:
                m_out[...] = m_in[...]
                l_out[...] = l_in[...]
                acc_out[...] = acc_in[...]

        if chunk == 2:
            compute()
        else:
            valid = first_row >= (2 - chunk) * rows
            pl.when(valid)(compute)
            pl.when(jnp.logical_not(valid))(passthrough)

    return kernel


def attend_chunk(chunk, queries, key_rows, value_rows, first_row, state):
    key_count, key_cols = key_rows.shape
    rows, query_cols = queries.shape
    kv_heads = key_cols // HEAD_DIM
    group = query_cols // key_cols
    heads = kv_heads * group
    first = state is None
    last = chunk == 0
    query_block = QUERY_BLOCK if chunk == 1 else MASKED_QUERY_BLOCK
    kernel = chunk_kernel(chunk, first, last, rows, key_count, query_block, group)
    q_spec = pl.BlockSpec((rows, group * HEAD_DIM), lambda h, f: (0, h))
    kv_spec = pl.BlockSpec((key_count, HEAD_DIM), lambda h, f: (0, h))
    stat_spec = pl.BlockSpec((rows, heads), lambda h, f: (0, 0))
    state_specs = [stat_spec, stat_spec, q_spec]
    in_specs = [q_spec, kv_spec, kv_spec] + ([] if first else state_specs)
    stat_shape = jax.ShapeDtypeStruct((rows, heads), jnp.float32)
    if last:
        out_specs = q_spec
        out_shape = jax.ShapeDtypeStruct((rows, query_cols), jnp.bfloat16)
    else:
        out_specs = state_specs
        out_shape = [stat_shape, stat_shape, jax.ShapeDtypeStruct((rows, query_cols), jnp.float32)]
    keys_per_row = rows // 2 + query_block // 2 if chunk != 1 else key_count
    cost = pl.CostEstimate(
        flops=4 * heads * rows * keys_per_row * HEAD_DIM,
        transcendentals=heads * rows * keys_per_row,
        bytes_accessed=rows * query_cols * (2 + 4 + (0 if first else 4)) + 4 * key_count * key_cols,
    )
    grid_spec = pltpu.PrefetchScalarGridSpec(
        num_scalar_prefetch=1,
        grid=(kv_heads,),
        in_specs=in_specs,
        out_specs=out_specs,
    )
    return pl.pallas_call(
        kernel,
        grid_spec=grid_spec,
        out_shape=out_shape,
        cost_estimate=cost,
        compiler_params=pltpu.CompilerParams(dimension_semantics=("arbitrary",)),
    )(first_row.reshape(1), queries, key_rows, value_rows, *([] if first else state))


def far_half_kernel(last, rows, key_rows, query_block, group):
    blocks = rows // query_block

    def kernel(scalar_ref, q_ref, k_ref, v_ref, m_in, l_in, acc_in, *outs):
        if last:
            (o_ref,) = outs
        else:
            m_out, l_out, acc_out = outs
        head = pl.program_id(0)
        first_row = scalar_ref[0]
        key_offset = scalar_ref[1]
        stat_cols = m_in.shape[1]
        lane = lax.broadcasted_iota(jnp.int32, (query_block, stat_cols), 1)
        shape = (query_block, key_rows)
        key_local = key_offset + lax.broadcasted_iota(jnp.int32, shape, 1)
        query_local = lax.broadcasted_iota(jnp.int32, shape, 0)
        head_cols = [slice(g * HEAD_DIM, (g + 1) * HEAD_DIM) for g in range(group)]
        picks = [lane == group * head + g for g in range(group)]

        def block_compute(r0):
            qrows = slice(r0, r0 + query_block)
            allowed = key_local > r0 + query_local
            m_block = m_in[qrows, :]
            l_block = l_in[qrows, :]
            if not last:
                m_keep = m_out[qrows, :]
                l_keep = l_out[qrows, :]
            for g, cols in enumerate(head_cols):
                s = lax.dot_general(
                    q_ref[qrows, cols], k_ref[...], (((1,), (1,)), ((), ())),
                    preferred_element_type=jnp.float32,
                ) * log2_scale
                s = jnp.where(allowed, s, masked_score)
                block_max = s.max(axis=1, keepdims=True)
                m_prev = jnp.sum(jnp.where(picks[g], m_block, 0.0), axis=1, keepdims=True)
                l_prev = jnp.sum(jnp.where(picks[g], l_block, 0.0), axis=1, keepdims=True)
                m_new = jnp.maximum(m_prev, block_max)
                alpha = jnp.exp2(m_prev - m_new)
                p = jnp.exp2(s - m_new)
                l_new = alpha * l_prev + p.sum(axis=1, keepdims=True)
                acc_new = alpha * acc_in[qrows, cols] + jnp.dot(
                    p.astype(jnp.bfloat16), v_ref[...], preferred_element_type=jnp.float32)
                if last:
                    o_ref[qrows, cols] = (acc_new / l_new).astype(o_ref.dtype)
                else:
                    acc_out[qrows, cols] = acc_new
                    m_keep = jnp.where(picks[g], m_new, m_keep)
                    l_keep = jnp.where(picks[g], l_new, l_keep)
            if not last:
                m_out[qrows, :] = m_keep
                l_out[qrows, :] = l_keep

        def block_pass(r0):
            qrows = slice(r0, r0 + query_block)
            m_block = m_in[qrows, :]
            l_block = l_in[qrows, :]
            if last:
                for g, cols in enumerate(head_cols):
                    l_prev = jnp.sum(jnp.where(picks[g], l_block, 0.0), axis=1, keepdims=True)
                    o_ref[qrows, cols] = (acc_in[qrows, cols] / l_prev).astype(o_ref.dtype)
            else:
                m_keep = m_out[qrows, :]
                l_keep = l_out[qrows, :]
                for g, cols in enumerate(head_cols):
                    m_keep = jnp.where(picks[g], m_block, m_keep)
                    l_keep = jnp.where(picks[g], l_block, l_keep)
                    acc_out[qrows, cols] = acc_in[qrows, cols]
                m_out[qrows, :] = m_keep
                l_out[qrows, :] = l_keep

        valid_chunk = first_row >= 2 * rows
        for block in range(blocks):
            r0 = block * query_block
            useful = valid_chunk & (key_offset + key_rows - 1 > r0)
            pl.when(useful)(functools.partial(block_compute, r0))
            pl.when(jnp.logical_not(useful))(functools.partial(block_pass, r0))

    return kernel


def attend_far_half(queries, key_rows, value_rows, first_row, key_offset, state, last):
    key_count, key_cols = key_rows.shape
    rows, query_cols = queries.shape
    kv_heads = key_cols // HEAD_DIM
    group = query_cols // key_cols
    heads = kv_heads * group
    kernel = far_half_kernel(last, rows, key_count, MASKED_QUERY_BLOCK, group)
    q_spec = pl.BlockSpec((rows, group * HEAD_DIM), lambda h, f: (0, h))
    kv_spec = pl.BlockSpec((key_count, HEAD_DIM), lambda h, f: (0, h))
    stat_spec = pl.BlockSpec((rows, heads), lambda h, f: (0, 0))
    state_specs = [stat_spec, stat_spec, q_spec]
    stat_shape = jax.ShapeDtypeStruct((rows, heads), jnp.float32)
    if last:
        out_specs = q_spec
        out_shape = jax.ShapeDtypeStruct((rows, query_cols), jnp.bfloat16)
    else:
        out_specs = state_specs
        out_shape = [stat_shape, stat_shape, jax.ShapeDtypeStruct((rows, query_cols), jnp.float32)]
    cost = pl.CostEstimate(
        flops=4 * heads * rows * key_count * HEAD_DIM,
        transcendentals=heads * rows * key_count,
        bytes_accessed=rows * query_cols * (2 + 4 + 4) + 4 * key_count * key_cols,
    )
    grid_spec = pltpu.PrefetchScalarGridSpec(
        num_scalar_prefetch=1,
        grid=(kv_heads,),
        in_specs=[q_spec, kv_spec, kv_spec] + state_specs,
        out_specs=out_specs,
    )
    scalars = jnp.stack([first_row, key_offset]).astype(jnp.int32)
    return pl.pallas_call(
        kernel,
        grid_spec=grid_spec,
        out_shape=out_shape,
        cost_estimate=cost,
        compiler_params=pltpu.CompilerParams(dimension_semantics=("arbitrary",)),
    )(scalars, queries, key_rows, value_rows, *state)


def swap_variant(half):
    variants = lax.axis_size("variant")
    return lax.ppermute(half, "variant", [(i, (i + 1) % variants) for i in range(variants)])


def halves_in_order(own, other, variant_index):
    return jnp.where(
        variant_index == 0,
        jnp.concatenate([own, other], axis=1),
        jnp.concatenate([other, own], axis=1),
    )


def shard_body(queries, keys, values, clean_keys, clean_values, owner_shard, span_offset, span_length):
    row_count = keys.shape[0]
    assert WINDOW == 2 * row_count
    shard_index = lax.axis_index("seq")
    first_row = (shard_index * row_count).astype(jnp.int32)
    position = lax.broadcasted_iota(jnp.int32, (row_count, span_offset.shape[1]), 0)
    in_span = (position >= span_offset) & (position < span_offset + span_length)
    in_span = in_span & (owner_shard[:, None] == shard_index)
    inside = jnp.any(in_span, axis=1)
    corrupt_pair = jnp.stack([keys, values])
    clean_own = jnp.stack([clean_keys, clean_values])
    if lax.axis_size("variant") != 2:
        clean_full = lax.all_gather(clean_own, "variant", axis=1, tiled=True)
        patched = jnp.where(inside[None, :, None], clean_full, corrupt_pair)
        near = shifted(patched, "seq", 1)
        far = shifted(near, "seq", 1)
        near_parts = (near,)
        far_parts = None
    else:
        half = row_count // 2
        variant_index = lax.axis_index("variant")
        lo, hi = corrupt_pair[:, :half], corrupt_pair[:, half:]
        inside_lo, inside_hi = inside[:half], inside[half:]
        corrupt_own = jnp.where(variant_index == 0, lo, hi)
        corrupt_other = jnp.where(variant_index == 0, hi, lo)
        inside_own = jnp.where(variant_index == 0, inside_lo, inside_hi)
        inside_other = jnp.where(variant_index == 0, inside_hi, inside_lo)
        own_half = jnp.where(inside_own[None, :, None], clean_own, corrupt_own)
        own_half, clean_own = lax.optimization_barrier((own_half, clean_own))
        near_own = shifted(own_half, "seq", 1)
        clean_other = swap_variant(clean_own)
        other_half = jnp.where(inside_other[None, :, None], clean_other, corrupt_other)
        near_other = shifted(other_half, "seq", 1)
        far_own = shifted(near_own, "seq", 1)
        far_other = shifted(near_other, "seq", 1)
        patched = halves_in_order(own_half, other_half, variant_index)
        near_parts = (near_own, near_other)
        far_parts = ((far_own, half * variant_index), (far_other, half * (1 - variant_index)))
    state = attend_chunk(2, queries, patched[0], patched[1], first_row, None)
    for part in near_parts:
        state = attend_chunk(1, queries, part[0], part[1], first_row, state)
    if far_parts is None:
        result = attend_chunk(0, queries, far[0], far[1], first_row, state)
    else:
        for part_index, (part, offset) in enumerate(far_parts):
            state = attend_far_half(queries, part[0], part[1], first_row, offset, state,
                                    part_index == len(far_parts) - 1)
        result = state
    return result[None]


def solution(mesh):
    placed = (
        P(("groups", "seq"), "mp"),
        P(("groups", "seq"), "mp"),
        P(("groups", "seq"), "mp"),
        P(("groups", "seq", "variant"), "mp"),
        P(("groups", "seq", "variant"), "mp"),
        P(("groups", "variant")),
        P(("groups", "variant"), None),
        P(("groups", "variant"), None),
    )
    return jax.shard_map(
        shard_body,
        mesh=mesh,
        in_specs=placed,
        out_specs=P("variant", ("groups", "seq"), "mp"),
        check_vma=False,
    )
```

```python
import jax
import jax.numpy as jnp
from jax import lax
from jax.experimental import pallas as pl
from jax.experimental.pallas import tpu as pltpu
from jax.sharding import PartitionSpec as P


HEAD_DIM = 128
WINDOW = 1024
QUERY_BLOCK = 512
MASKED_QUERY_BLOCK = 512

query_scale = 168.0 ** (-0.5)
log2_scale = query_scale * 1.4426950408889634
masked_score = -1e30


def shifted(shard, axis, by):
    devices = lax.axis_size(axis)
    pairs = [(i, i + by) for i in range(devices) if 0 <= i + by < devices]
    return lax.ppermute(shard, axis, pairs)


def row_reduce(x, combine, reduce):
    lanes = 128
    partial = x[:, :lanes]
    for start in range(lanes, x.shape[1], lanes):
        partial = combine(partial, x[:, start:start + lanes])
    return reduce(partial, axis=1, keepdims=True)


def chunk_kernel(chunk, first, last, rows, key_rows, query_block, group):
    blocks = rows // query_block

    def kernel(first_ref, q_ref, k_ref, v_ref, *rest):
        if first:
            m_out, l_out, acc_out = rest
        elif last:
            m_in, l_in, acc_in, o_ref = rest
        else:
            m_in, l_in, acc_in, m_out, l_out, acc_out = rest
        head = pl.program_id(0)
        first_row = first_ref[0]
        stat_cols = (m_out if first else m_in).shape[1]
        diag_shape = (query_block, query_block)
        diag_row = lax.broadcasted_iota(jnp.int32, diag_shape, 0)
        diag_col = lax.broadcasted_iota(jnp.int32, diag_shape, 1)
        diag_allowed = diag_col <= diag_row if chunk == 2 else diag_col > diag_row
        lane = lax.broadcasted_iota(jnp.int32, (query_block, stat_cols), 1)

        def compute():
            for block in range(blocks):
                r0 = block * query_block
                if chunk == 2:
                    pieces = [(0, r0, False), (r0, r0 + query_block, True)]
                elif chunk == 1:
                    pieces = [(0, key_rows, False)]
                else:
                    pieces = [(r0, r0 + query_block, True), (r0 + query_block, rows, False)]
                pieces = [piece for piece in pieces if piece[1] > piece[0]]
                qrows = slice(r0, r0 + query_block)
                if not first:
                    m_block = m_in[qrows, :]
                    l_block = l_in[qrows, :]
                if not last:
                    m_keep = m_out[qrows, :]
                    l_keep = l_out[qrows, :]
                for g in range(group):
                    pick = lane == group * head + g
                    cols = slice(g * HEAD_DIM, (g + 1) * HEAD_DIM)
                    query = q_ref[qrows, cols]
                    scores = []
                    for k0, k1, masked in pieces:
                        s = lax.dot_general(
                            query, k_ref[k0:k1, :], (((1,), (1,)), ((), ())),
                            preferred_element_type=jnp.float32,
                        ) * log2_scale
                        if masked:
                            s = jnp.where(diag_allowed, s, masked_score)
                        scores.append(s)
                    block_max = row_reduce(jnp.concatenate(scores, axis=1) if len(scores) > 1 else scores[0],
                                           jnp.maximum, jnp.max)
                    if first:
                        m_new = block_max
                    else:
                        m_prev = jnp.sum(jnp.where(pick, m_block, 0.0), axis=1, keepdims=True)
                        l_prev = jnp.sum(jnp.where(pick, l_block, 0.0), axis=1, keepdims=True)
                        m_new = jnp.maximum(m_prev, block_max)
                        alpha = jnp.exp2(m_prev - m_new)
                    l_part = None
                    pv = None
                    for (k0, k1, masked), s in zip(pieces, scores):
                        p = jnp.exp2(s - m_new)
                        part = row_reduce(p, jnp.add, jnp.sum)
                        l_part = part if l_part is None else l_part + part
                        term = jnp.dot(p.astype(jnp.bfloat16), v_ref[k0:k1, :],
                                       preferred_element_type=jnp.float32)
                        pv = term if pv is None else pv + term
                    if first:
                        l_new = l_part
                        acc_new = pv
                    else:
                        l_new = alpha * l_prev + l_part
                        acc_new = alpha * acc_in[qrows, cols] + pv
                    if last:
                        o_ref[qrows, cols] = (acc_new / l_new).astype(o_ref.dtype)
                    else:
                        acc_out[qrows, cols] = acc_new
                        m_keep = jnp.where(pick, m_new, m_keep)
                        l_keep = jnp.where(pick, l_new, l_keep)
                if not last:
                    m_out[qrows, :] = m_keep
                    l_out[qrows, :] = l_keep

        def passthrough():
            if last:
                all_lanes = lax.broadcasted_iota(jnp.int32, (rows, stat_cols), 1)
                l_all = l_in[...]
                for g in range(group):
                    cols = slice(g * HEAD_DIM, (g + 1) * HEAD_DIM)
                    l_prev = jnp.sum(jnp.where(all_lanes == group * head + g, l_all, 0.0),
                                     axis=1, keepdims=True)
                    o_ref[:, cols] = (acc_in[:, cols] / l_prev).astype(o_ref.dtype)
            else:
                m_out[...] = m_in[...]
                l_out[...] = l_in[...]
                acc_out[...] = acc_in[...]

        if chunk == 2:
            compute()
        else:
            valid = first_row >= (2 - chunk) * rows
            pl.when(valid)(compute)
            pl.when(jnp.logical_not(valid))(passthrough)

    return kernel


def attend_chunk(chunk, queries, key_rows, value_rows, first_row, state):
    key_count, key_cols = key_rows.shape
    rows, query_cols = queries.shape
    kv_heads = key_cols // HEAD_DIM
    group = query_cols // key_cols
    heads = kv_heads * group
    first = state is None
    last = chunk == 0
    query_block = QUERY_BLOCK if chunk == 1 else MASKED_QUERY_BLOCK
    kernel = chunk_kernel(chunk, first, last, rows, key_count, query_block, group)
    q_spec = pl.BlockSpec((rows, group * HEAD_DIM), lambda h, f: (0, h))
    kv_spec = pl.BlockSpec((key_count, HEAD_DIM), lambda h, f: (0, h))
    stat_spec = pl.BlockSpec((rows, heads), lambda h, f: (0, 0))
    state_specs = [stat_spec, stat_spec, q_spec]
    in_specs = [q_spec, kv_spec, kv_spec] + ([] if first else state_specs)
    stat_shape = jax.ShapeDtypeStruct((rows, heads), jnp.float32)
    if last:
        out_specs = q_spec
        out_shape = jax.ShapeDtypeStruct((rows, query_cols), jnp.bfloat16)
    else:
        out_specs = state_specs
        out_shape = [stat_shape, stat_shape, jax.ShapeDtypeStruct((rows, query_cols), jnp.float32)]
    keys_per_row = rows // 2 + query_block // 2 if chunk != 1 else key_count
    cost = pl.CostEstimate(
        flops=4 * heads * rows * keys_per_row * HEAD_DIM,
        transcendentals=heads * rows * keys_per_row,
        bytes_accessed=rows * query_cols * (2 + 4 + (0 if first else 4)) + 4 * key_count * key_cols,
    )
    grid_spec = pltpu.PrefetchScalarGridSpec(
        num_scalar_prefetch=1,
        grid=(kv_heads,),
        in_specs=in_specs,
        out_specs=out_specs,
    )
    return pl.pallas_call(
        kernel,
        grid_spec=grid_spec,
        out_shape=out_shape,
        cost_estimate=cost,
        compiler_params=pltpu.CompilerParams(dimension_semantics=("arbitrary",)),
    )(first_row.reshape(1), queries, key_rows, value_rows, *([] if first else state))


def swap_variant(half):
    variants = lax.axis_size("variant")
    return lax.ppermute(half, "variant", [(i, (i + 1) % variants) for i in range(variants)])


def halves_in_order(own, other, variant_index):
    return jnp.where(
        variant_index == 0,
        jnp.concatenate([own, other], axis=1),
        jnp.concatenate([other, own], axis=1),
    )


def shard_body(queries, keys, values, clean_keys, clean_values, owner_shard, span_offset, span_length):
    row_count = keys.shape[0]
    assert WINDOW == 2 * row_count
    shard_index = lax.axis_index("seq")
    first_row = (shard_index * row_count).astype(jnp.int32)
    position = lax.broadcasted_iota(jnp.int32, (row_count, span_offset.shape[1]), 0)
    in_span = (position >= span_offset) & (position < span_offset + span_length)
    in_span = in_span & (owner_shard[:, None] == shard_index)
    inside = jnp.any(in_span, axis=1)
    corrupt_pair = jnp.stack([keys, values])
    clean_own = jnp.stack([clean_keys, clean_values])
    if lax.axis_size("variant") != 2:
        clean_full = lax.all_gather(clean_own, "variant", axis=1, tiled=True)
        patched = jnp.where(inside[None, :, None], clean_full, corrupt_pair)
        near = shifted(patched, "seq", 1)
        far = shifted(near, "seq", 1)
        near_parts = (near,)
    else:
        half = row_count // 2
        variant_index = lax.axis_index("variant")
        lo, hi = corrupt_pair[:, :half], corrupt_pair[:, half:]
        inside_lo, inside_hi = inside[:half], inside[half:]
        corrupt_own = jnp.where(variant_index == 0, lo, hi)
        corrupt_other = jnp.where(variant_index == 0, hi, lo)
        inside_own = jnp.where(variant_index == 0, inside_lo, inside_hi)
        inside_other = jnp.where(variant_index == 0, inside_hi, inside_lo)
        own_half = jnp.where(inside_own[None, :, None], clean_own, corrupt_own)
        own_half, clean_own = lax.optimization_barrier((own_half, clean_own))
        near_own = shifted(own_half, "seq", 1)
        clean_other = swap_variant(clean_own)
        other_half = jnp.where(inside_other[None, :, None], clean_other, corrupt_other)
        near_other = shifted(other_half, "seq", 1)
        far_own = shifted(near_own, "seq", 1)
        far_other = shifted(near_other, "seq", 1)
        patched = halves_in_order(own_half, other_half, variant_index)
        far = halves_in_order(far_own, far_other, variant_index)
        near_parts = (near_own, near_other)
    state = attend_chunk(2, queries, patched[0], patched[1], first_row, None)
    for part in near_parts:
        state = attend_chunk(1, queries, part[0], part[1], first_row, state)
    result = attend_chunk(0, queries, far[0], far[1], first_row, state)
    return result[None]


def solution(mesh):
    placed = (
        P(("groups", "seq"), "mp"),
        P(("groups", "seq"), "mp"),
        P(("groups", "seq"), "mp"),
        P(("groups", "seq", "variant"), "mp"),
        P(("groups", "seq", "variant"), "mp"),
        P(("groups", "variant")),
        P(("groups", "variant"), None),
        P(("groups", "variant"), None),
    )
    return jax.shard_map(
        shard_body,
        mesh=mesh,
        in_specs=placed,
        out_specs=P("variant", ("groups", "seq"), "mp"),
        check_vma=False,
    )
```

```python
import jax
import jax.numpy as jnp
from jax import lax
from jax.experimental import pallas as pl
from jax.experimental.pallas import tpu as pltpu
from jax.sharding import PartitionSpec as P


HEAD_DIM = 128
WINDOW = 1024
QUERY_BLOCK = 512
MASKED_QUERY_BLOCK = 512

query_scale = 168.0 ** (-0.5)
log2_scale = query_scale * 1.4426950408889634
masked_score = -1e30


def shifted(shard, axis, by):
    devices = lax.axis_size(axis)
    pairs = [(i, i + by) for i in range(devices) if 0 <= i + by < devices]
    return lax.ppermute(shard, axis, pairs)


def row_reduce(x, combine, reduce):
    lanes = 128
    partial = x[:, :lanes]
    for start in range(lanes, x.shape[1], lanes):
        partial = combine(partial, x[:, start:start + lanes])
    return reduce(partial, axis=1, keepdims=True)


def chunk_kernel(chunk, first, last, rows, key_rows, query_block, group, split):
    blocks = rows // query_block

    def kernel(first_ref, q_ref, *rest):
        if split:
            ka_ref, va_ref, kb_ref, vb_ref = rest[:4]
            rest = rest[4:]
            swap = first_ref[1] != 0
            ka, kb, va, vb = ka_ref[...], kb_ref[...], va_ref[...], vb_ref[...]
            keys_all = jnp.concatenate([jnp.where(swap, kb, ka), jnp.where(swap, ka, kb)], axis=0)
            values_all = jnp.concatenate([jnp.where(swap, vb, va), jnp.where(swap, va, vb)], axis=0)
            get_keys = lambda k0, k1: keys_all[k0:k1]
            get_values = lambda k0, k1: values_all[k0:k1]
        else:
            k_ref, v_ref = rest[:2]
            rest = rest[2:]
            get_keys = lambda k0, k1: k_ref[k0:k1, :]
            get_values = lambda k0, k1: v_ref[k0:k1, :]
        if first:
            m_out, l_out, acc_out = rest
        elif last:
            m_in, l_in, acc_in, o_ref = rest
        else:
            m_in, l_in, acc_in, m_out, l_out, acc_out = rest
        head = pl.program_id(0)
        first_row = first_ref[0]
        stat_cols = (m_out if first else m_in).shape[1]
        diag_shape = (query_block, query_block)
        diag_row = lax.broadcasted_iota(jnp.int32, diag_shape, 0)
        diag_col = lax.broadcasted_iota(jnp.int32, diag_shape, 1)
        diag_allowed = diag_col <= diag_row if chunk == 2 else diag_col > diag_row
        lane = lax.broadcasted_iota(jnp.int32, (query_block, stat_cols), 1)

        def compute():
            for block in range(blocks):
                r0 = block * query_block
                if chunk == 2:
                    pieces = [(0, r0, False), (r0, r0 + query_block, True)]
                elif chunk == 1:
                    pieces = [(0, key_rows, False)]
                else:
                    pieces = [(r0, r0 + query_block, True), (r0 + query_block, rows, False)]
                pieces = [piece for piece in pieces if piece[1] > piece[0]]
                qrows = slice(r0, r0 + query_block)
                if not first:
                    m_block = m_in[qrows, :]
                    l_block = l_in[qrows, :]
                if not last:
                    m_keep = m_out[qrows, :]
                    l_keep = l_out[qrows, :]
                for g in range(group):
                    pick = lane == group * head + g
                    cols = slice(g * HEAD_DIM, (g + 1) * HEAD_DIM)
                    query = q_ref[qrows, cols]
                    scores = []
                    for k0, k1, masked in pieces:
                        s = lax.dot_general(
                            query, get_keys(k0, k1), (((1,), (1,)), ((), ())),
                            preferred_element_type=jnp.float32,
                        ) * log2_scale
                        if masked:
                            s = jnp.where(diag_allowed, s, masked_score)
                        scores.append(s)
                    block_max = row_reduce(jnp.concatenate(scores, axis=1) if len(scores) > 1 else scores[0],
                                           jnp.maximum, jnp.max)
                    if first:
                        m_new = block_max
                    else:
                        m_prev = jnp.sum(jnp.where(pick, m_block, 0.0), axis=1, keepdims=True)
                        l_prev = jnp.sum(jnp.where(pick, l_block, 0.0), axis=1, keepdims=True)
                        m_new = jnp.maximum(m_prev, block_max)
                        alpha = jnp.exp2(m_prev - m_new)
                    l_part = None
                    pv = None
                    for (k0, k1, masked), s in zip(pieces, scores):
                        p = jnp.exp2(s - m_new)
                        part = row_reduce(p, jnp.add, jnp.sum)
                        l_part = part if l_part is None else l_part + part
                        term = jnp.dot(p.astype(jnp.bfloat16), get_values(k0, k1),
                                       preferred_element_type=jnp.float32)
                        pv = term if pv is None else pv + term
                    if first:
                        l_new = l_part
                        acc_new = pv
                    else:
                        l_new = alpha * l_prev + l_part
                        acc_new = alpha * acc_in[qrows, cols] + pv
                    if last:
                        o_ref[qrows, cols] = (acc_new / l_new).astype(o_ref.dtype)
                    else:
                        acc_out[qrows, cols] = acc_new
                        m_keep = jnp.where(pick, m_new, m_keep)
                        l_keep = jnp.where(pick, l_new, l_keep)
                if not last:
                    m_out[qrows, :] = m_keep
                    l_out[qrows, :] = l_keep

        def passthrough():
            if last:
                all_lanes = lax.broadcasted_iota(jnp.int32, (rows, stat_cols), 1)
                l_all = l_in[...]
                for g in range(group):
                    cols = slice(g * HEAD_DIM, (g + 1) * HEAD_DIM)
                    l_prev = jnp.sum(jnp.where(all_lanes == group * head + g, l_all, 0.0),
                                     axis=1, keepdims=True)
                    o_ref[:, cols] = (acc_in[:, cols] / l_prev).astype(o_ref.dtype)
            else:
                m_out[...] = m_in[...]
                l_out[...] = l_in[...]
                acc_out[...] = acc_in[...]

        if chunk == 2:
            compute()
        else:
            valid = first_row >= (2 - chunk) * rows
            pl.when(valid)(compute)
            pl.when(jnp.logical_not(valid))(passthrough)

    return kernel


def attend_chunk(chunk, queries, pair, first_row, state, other=None, swap=None):
    split = other is not None
    key_count, key_cols = pair.shape[1:]
    rows, query_cols = queries.shape
    kv_heads = key_cols // HEAD_DIM
    group = query_cols // key_cols
    heads = kv_heads * group
    first = state is None
    last = chunk == 0
    query_block = QUERY_BLOCK if chunk == 1 else MASKED_QUERY_BLOCK
    kernel = chunk_kernel(chunk, first, last, rows, key_count * (2 if split else 1), query_block, group, split)
    q_spec = pl.BlockSpec((rows, group * HEAD_DIM), lambda h, f: (0, h))
    k_spec = pl.BlockSpec((None, key_count, HEAD_DIM), lambda h, f: (0, 0, h))
    v_spec = pl.BlockSpec((None, key_count, HEAD_DIM), lambda h, f: (1, 0, h))
    stat_spec = pl.BlockSpec((rows, heads), lambda h, f: (0, 0))
    state_specs = [stat_spec, stat_spec, q_spec]
    in_specs = [q_spec, k_spec, v_spec] + ([k_spec, v_spec] if split else []) + ([] if first else state_specs)
    stat_shape = jax.ShapeDtypeStruct((rows, heads), jnp.float32)
    if last:
        out_specs = q_spec
        out_shape = jax.ShapeDtypeStruct((rows, query_cols), jnp.bfloat16)
    else:
        out_specs = state_specs
        out_shape = [stat_shape, stat_shape, jax.ShapeDtypeStruct((rows, query_cols), jnp.float32)]
    keys_per_row = rows // 2 + query_block // 2 if chunk != 1 else key_count
    cost = pl.CostEstimate(
        flops=4 * heads * rows * keys_per_row * HEAD_DIM,
        transcendentals=heads * rows * keys_per_row,
        bytes_accessed=rows * query_cols * (2 + 4 + (0 if first else 4)) + 4 * key_count * key_cols,
    )
    grid_spec = pltpu.PrefetchScalarGridSpec(
        num_scalar_prefetch=1,
        grid=(kv_heads,),
        in_specs=in_specs,
        out_specs=out_specs,
    )
    scalars = jnp.stack([first_row, swap]).astype(jnp.int32) if split else first_row.reshape(1)
    pairs = (pair, pair, other, other) if split else (pair, pair)
    return pl.pallas_call(
        kernel,
        grid_spec=grid_spec,
        out_shape=out_shape,
        cost_estimate=cost,
        compiler_params=pltpu.CompilerParams(dimension_semantics=("arbitrary",)),
    )(scalars, queries, *pairs, *([] if first else state))


def swap_variant(half):
    variants = lax.axis_size("variant")
    return lax.ppermute(half, "variant", [(i, (i + 1) % variants) for i in range(variants)])


def halves_in_order(own, other, variant_index):
    return jnp.where(
        variant_index == 0,
        jnp.concatenate([own, other], axis=1),
        jnp.concatenate([other, own], axis=1),
    )


def shard_body(queries, keys, values, clean_keys, clean_values, owner_shard, span_offset, span_length):
    row_count = keys.shape[0]
    assert WINDOW == 2 * row_count
    shard_index = lax.axis_index("seq")
    first_row = (shard_index * row_count).astype(jnp.int32)
    position = lax.broadcasted_iota(jnp.int32, (row_count, span_offset.shape[1]), 0)
    in_span = (position >= span_offset) & (position < span_offset + span_length)
    in_span = in_span & (owner_shard[:, None] == shard_index)
    inside = jnp.any(in_span, axis=1)
    corrupt_pair = jnp.stack([keys, values])
    clean_own = jnp.stack([clean_keys, clean_values])
    if lax.axis_size("variant") != 2:
        clean_full = lax.all_gather(clean_own, "variant", axis=1, tiled=True)
        patched = jnp.where(inside[None, :, None], clean_full, corrupt_pair)
        near = shifted(patched, "seq", 1)
        far = shifted(near, "seq", 1)
        near_parts = (near,)
    else:
        half = row_count // 2
        variant_index = lax.axis_index("variant")
        lo, hi = corrupt_pair[:, :half], corrupt_pair[:, half:]
        inside_lo, inside_hi = inside[:half], inside[half:]
        corrupt_own = jnp.where(variant_index == 0, lo, hi)
        corrupt_other = jnp.where(variant_index == 0, hi, lo)
        inside_own = jnp.where(variant_index == 0, inside_lo, inside_hi)
        inside_other = jnp.where(variant_index == 0, inside_hi, inside_lo)
        own_half = jnp.where(inside_own[None, :, None], clean_own, corrupt_own)
        own_half, clean_own = lax.optimization_barrier((own_half, clean_own))
        near_own = shifted(own_half, "seq", 1)
        clean_other = swap_variant(clean_own)
        other_half = jnp.where(inside_other[None, :, None], clean_other, corrupt_other)
        near_other = shifted(other_half, "seq", 1)
        far_own = shifted(near_own, "seq", 1)
        far_other = shifted(near_other, "seq", 1)
        patched = halves_in_order(own_half, other_half, variant_index)
        near_parts = (near_own, near_other)
        far = None
    state = attend_chunk(2, queries, patched, first_row, None)
    for part in near_parts:
        state = attend_chunk(1, queries, part, first_row, state)
    if far is None:
        result = attend_chunk(0, queries, far_own, first_row, state, far_other, variant_index)
    else:
        result = attend_chunk(0, queries, far, first_row, state)
    return result[None]


def solution(mesh):
    placed = (
        P(("groups", "seq"), "mp"),
        P(("groups", "seq"), "mp"),
        P(("groups", "seq"), "mp"),
        P(("groups", "seq", "variant"), "mp"),
        P(("groups", "seq", "variant"), "mp"),
        P(("groups", "variant")),
        P(("groups", "variant"), None),
        P(("groups", "variant"), None),
    )
    return jax.shard_map(
        shard_body,
        mesh=mesh,
        in_specs=placed,
        out_specs=P("variant", ("groups", "seq"), "mp"),
        check_vma=False,
    )
```

```python
import jax
import jax.numpy as jnp
from jax import lax
from jax.experimental import pallas as pl
from jax.experimental.pallas import tpu as pltpu
from jax.sharding import PartitionSpec as P


HEAD_DIM = 128
WINDOW = 1024
QUERY_BLOCK = 512
MASKED_QUERY_BLOCK = 512

query_scale = 168.0 ** (-0.5)
log2_scale = query_scale * 1.4426950408889634
masked_score = -1e30


def shifted(shard, axis, by):
    devices = lax.axis_size(axis)
    pairs = [(i, i + by) for i in range(devices) if 0 <= i + by < devices]
    return lax.ppermute(shard, axis, pairs)


def row_reduce(x, combine, reduce):
    lanes = 128
    partial = x[:, :lanes]
    for start in range(lanes, x.shape[1], lanes):
        partial = combine(partial, x[:, start:start + lanes])
    return reduce(partial, axis=1, keepdims=True)


def chunk_kernel(chunk, first, last, rows, key_rows, query_block, group, head_base=0, aliased=False):
    blocks = rows // query_block

    def kernel(first_ref, q_ref, k_ref, v_ref, *rest):
        if aliased:
            rest = rest[:-2] + rest[-1:]
        if first:
            m_out, l_out, acc_out = rest
        elif last:
            m_in, l_in, acc_in, o_ref = rest
        else:
            m_in, l_in, acc_in, m_out, l_out, acc_out = rest
        head = pl.program_id(0) + head_base
        first_row = first_ref[0]
        stat_cols = (m_out if first else m_in).shape[1]
        diag_shape = (query_block, query_block)
        diag_row = lax.broadcasted_iota(jnp.int32, diag_shape, 0)
        diag_col = lax.broadcasted_iota(jnp.int32, diag_shape, 1)
        diag_allowed = diag_col <= diag_row if chunk == 2 else diag_col > diag_row
        lane = lax.broadcasted_iota(jnp.int32, (query_block, stat_cols), 1)

        def compute():
            for block in range(blocks):
                r0 = block * query_block
                if chunk == 2:
                    pieces = [(0, r0, False), (r0, r0 + query_block, True)]
                elif chunk == 1:
                    pieces = [(0, key_rows, False)]
                else:
                    pieces = [(r0, r0 + query_block, True), (r0 + query_block, rows, False)]
                pieces = [piece for piece in pieces if piece[1] > piece[0]]
                qrows = slice(r0, r0 + query_block)
                if not first:
                    m_block = m_in[qrows, :]
                    l_block = l_in[qrows, :]
                if not last:
                    m_keep = m_out[qrows, :]
                    l_keep = l_out[qrows, :]
                for g in range(group):
                    pick = lane == group * head + g
                    cols = slice(g * HEAD_DIM, (g + 1) * HEAD_DIM)
                    query = q_ref[qrows, cols]
                    scores = []
                    for k0, k1, masked in pieces:
                        s = lax.dot_general(
                            query, k_ref[k0:k1, :], (((1,), (1,)), ((), ())),
                            preferred_element_type=jnp.float32,
                        ) * log2_scale
                        if masked:
                            s = jnp.where(diag_allowed, s, masked_score)
                        scores.append(s)
                    block_max = row_reduce(jnp.concatenate(scores, axis=1) if len(scores) > 1 else scores[0],
                                           jnp.maximum, jnp.max)
                    if first:
                        m_new = block_max
                    else:
                        m_prev = jnp.sum(jnp.where(pick, m_block, 0.0), axis=1, keepdims=True)
                        l_prev = jnp.sum(jnp.where(pick, l_block, 0.0), axis=1, keepdims=True)
                        m_new = jnp.maximum(m_prev, block_max)
                        alpha = jnp.exp2(m_prev - m_new)
                    l_part = None
                    pv = None
                    for (k0, k1, masked), s in zip(pieces, scores):
                        p = jnp.exp2(s - m_new)
                        part = row_reduce(p, jnp.add, jnp.sum)
                        l_part = part if l_part is None else l_part + part
                        term = jnp.dot(p.astype(jnp.bfloat16), v_ref[k0:k1, :],
                                       preferred_element_type=jnp.float32)
                        pv = term if pv is None else pv + term
                    if first:
                        l_new = l_part
                        acc_new = pv
                    else:
                        l_new = alpha * l_prev + l_part
                        acc_new = alpha * acc_in[qrows, cols] + pv
                    if last:
                        o_ref[qrows, cols] = (acc_new / l_new).astype(o_ref.dtype)
                    else:
                        acc_out[qrows, cols] = acc_new
                        m_keep = jnp.where(pick, m_new, m_keep)
                        l_keep = jnp.where(pick, l_new, l_keep)
                if not last:
                    m_out[qrows, :] = m_keep
                    l_out[qrows, :] = l_keep

        def passthrough():
            if last:
                all_lanes = lax.broadcasted_iota(jnp.int32, (rows, stat_cols), 1)
                l_all = l_in[...]
                for g in range(group):
                    cols = slice(g * HEAD_DIM, (g + 1) * HEAD_DIM)
                    l_prev = jnp.sum(jnp.where(all_lanes == group * head + g, l_all, 0.0),
                                     axis=1, keepdims=True)
                    o_ref[:, cols] = (acc_in[:, cols] / l_prev).astype(o_ref.dtype)
            else:
                m_out[...] = m_in[...]
                l_out[...] = l_in[...]
                acc_out[...] = acc_in[...]

        if chunk == 2:
            compute()
        else:
            valid = first_row >= (2 - chunk) * rows
            pl.when(valid)(compute)
            pl.when(jnp.logical_not(valid))(passthrough)

    return kernel


def attend_chunk(chunk, queries, pair, first_row, state, kv_total=None, head_base=0, alias=None):
    key_count, key_cols = pair.shape[1:]
    rows, query_cols = queries.shape
    kv_heads = key_cols // HEAD_DIM
    kv_total = kv_heads if kv_total is None else kv_total
    group = query_cols // (kv_total * HEAD_DIM)
    heads = kv_total * group
    first = state is None
    last = chunk == 0
    query_block = QUERY_BLOCK if chunk == 1 else MASKED_QUERY_BLOCK
    kernel = chunk_kernel(chunk, first, last, rows, key_count, query_block, group,
                          head_base, alias is not None)
    q_spec = pl.BlockSpec((rows, group * HEAD_DIM), lambda h, f: (0, h + head_base))
    k_spec = pl.BlockSpec((None, key_count, HEAD_DIM), lambda h, f: (0, 0, h))
    v_spec = pl.BlockSpec((None, key_count, HEAD_DIM), lambda h, f: (1, 0, h))
    stat_spec = pl.BlockSpec((rows, heads), lambda h, f: (0, 0))
    state_specs = [stat_spec, stat_spec, q_spec]
    in_specs = [q_spec, k_spec, v_spec] + ([] if first else state_specs)
    operands = [first_row.reshape(1), queries, pair, pair] + ([] if first else list(state))
    aliases = {}
    if alias is not None:
        in_specs.append(pl.BlockSpec(memory_space=pl.ANY))
        aliases = {len(operands): 0}
        operands.append(alias)
    stat_shape = jax.ShapeDtypeStruct((rows, heads), jnp.float32)
    if last:
        out_specs = q_spec
        out_shape = jax.ShapeDtypeStruct((rows, query_cols), jnp.bfloat16)
    else:
        out_specs = state_specs
        out_shape = [stat_shape, stat_shape, jax.ShapeDtypeStruct((rows, query_cols), jnp.float32)]
    keys_per_row = rows // 2 + query_block // 2 if chunk != 1 else key_count
    cost = pl.CostEstimate(
        flops=4 * kv_heads * group * rows * keys_per_row * HEAD_DIM,
        transcendentals=kv_heads * group * rows * keys_per_row,
        bytes_accessed=rows * kv_heads * group * HEAD_DIM * (2 + 4 + (0 if first else 4)) + 4 * key_count * key_cols,
    )
    grid_spec = pltpu.PrefetchScalarGridSpec(
        num_scalar_prefetch=1,
        grid=(kv_heads,),
        in_specs=in_specs,
        out_specs=out_specs,
    )
    return pl.pallas_call(
        kernel,
        grid_spec=grid_spec,
        out_shape=out_shape,
        cost_estimate=cost,
        input_output_aliases=aliases,
        compiler_params=pltpu.CompilerParams(dimension_semantics=("arbitrary",)),
    )(*operands)


def swap_variant(half):
    variants = lax.axis_size("variant")
    return lax.ppermute(half, "variant", [(i, (i + 1) % variants) for i in range(variants)])


def halves_in_order(own, other, variant_index):
    return jnp.where(
        variant_index == 0,
        jnp.concatenate([own, other], axis=1),
        jnp.concatenate([other, own], axis=1),
    )


def shard_body(queries, keys, values, clean_keys, clean_values, owner_shard, span_offset, span_length):
    row_count = keys.shape[0]
    assert WINDOW == 2 * row_count
    shard_index = lax.axis_index("seq")
    first_row = (shard_index * row_count).astype(jnp.int32)
    position = lax.broadcasted_iota(jnp.int32, (row_count, span_offset.shape[1]), 0)
    in_span = (position >= span_offset) & (position < span_offset + span_length)
    in_span = in_span & (owner_shard[:, None] == shard_index)
    inside = jnp.any(in_span, axis=1)
    corrupt_pair = jnp.stack([keys, values])
    clean_own = jnp.stack([clean_keys, clean_values])
    if lax.axis_size("variant") != 2:
        clean_full = lax.all_gather(clean_own, "variant", axis=1, tiled=True)
        patched = jnp.where(inside[None, :, None], clean_full, corrupt_pair)
        near = shifted(patched, "seq", 1)
        far = shifted(near, "seq", 1)
        near_parts = (near,)
    else:
        half = row_count // 2
        variant_index = lax.axis_index("variant")
        lo, hi = corrupt_pair[:, :half], corrupt_pair[:, half:]
        inside_lo, inside_hi = inside[:half], inside[half:]
        corrupt_own = jnp.where(variant_index == 0, lo, hi)
        corrupt_other = jnp.where(variant_index == 0, hi, lo)
        inside_own = jnp.where(variant_index == 0, inside_lo, inside_hi)
        inside_other = jnp.where(variant_index == 0, inside_hi, inside_lo)
        own_half = jnp.where(inside_own[None, :, None], clean_own, corrupt_own)
        own_half, clean_own = lax.optimization_barrier((own_half, clean_own))
        near_own = shifted(own_half, "seq", 1)
        clean_other = swap_variant(clean_own)
        other_half = jnp.where(inside_other[None, :, None], clean_other, corrupt_other)
        near_other = shifted(other_half, "seq", 1)
        far_own = shifted(near_own, "seq", 1)
        split_cols = keys.shape[1] // 2
        far_other_a = shifted(near_other[:, :, :split_cols], "seq", 1)
        far_other_b = shifted(near_other[:, :, split_cols:], "seq", 1)
        patched = halves_in_order(own_half, other_half, variant_index)
        far_a = halves_in_order(far_own[:, :, :split_cols], far_other_a, variant_index)
        far_b = halves_in_order(far_own[:, :, split_cols:], far_other_b, variant_index)
        far = None
        near_parts = (near_own, near_other)
    state = attend_chunk(2, queries, patched, first_row, None)
    for part in near_parts:
        state = attend_chunk(1, queries, part, first_row, state)
    if far is not None:
        result = attend_chunk(0, queries, far, first_row, state)
    else:
        kv_total = keys.shape[1] // HEAD_DIM
        partial = attend_chunk(0, queries, far_a, first_row, state, kv_total, 0)
        result = attend_chunk(0, queries, far_b, first_row, state, kv_total,
                              kv_total // 2, partial)
    return result[None]


def solution(mesh):
    placed = (
        P(("groups", "seq"), "mp"),
        P(("groups", "seq"), "mp"),
        P(("groups", "seq"), "mp"),
        P(("groups", "seq", "variant"), "mp"),
        P(("groups", "seq", "variant"), "mp"),
        P(("groups", "variant")),
        P(("groups", "variant"), None),
        P(("groups", "variant"), None),
    )
    return jax.shard_map(
        shard_body,
        mesh=mesh,
        in_specs=placed,
        out_specs=P("variant", ("groups", "seq"), "mp"),
        check_vma=False,
    )
```

```python
import jax
import jax.numpy as jnp
from jax import lax
from jax.experimental import pallas as pl
from jax.experimental.pallas import tpu as pltpu
from jax.sharding import PartitionSpec as P


HEAD_DIM = 128
WINDOW = 1024
QUERY_BLOCK = 512
MASKED_QUERY_BLOCK = 512

query_scale = 168.0 ** (-0.5)
log2_scale = query_scale * 1.4426950408889634
masked_score = -1e30


def shifted(shard, axis, by):
    devices = lax.axis_size(axis)
    pairs = [(i, i + by) for i in range(devices) if 0 <= i + by < devices]
    return lax.ppermute(shard, axis, pairs)


def row_reduce(x, combine, reduce):
    lanes = 128
    partial = x[:, :lanes]
    for start in range(lanes, x.shape[1], lanes):
        partial = combine(partial, x[:, start:start + lanes])
    return reduce(partial, axis=1, keepdims=True)


def chunk_kernel(chunk, first, last, rows, key_rows, query_block, group):
    blocks = rows // query_block

    def kernel(first_ref, q_ref, k_ref, v_ref, *rest):
        if first:
            m_out, l_out, acc_out = rest
        elif last:
            m_in, l_in, acc_in, o_ref = rest
        else:
            m_in, l_in, acc_in, m_out, l_out, acc_out = rest
        head = pl.program_id(0)
        first_row = first_ref[0]
        stat_cols = (m_out if first else m_in).shape[1]
        diag_shape = (query_block, query_block)
        diag_row = lax.broadcasted_iota(jnp.int32, diag_shape, 0)
        diag_col = lax.broadcasted_iota(jnp.int32, diag_shape, 1)
        diag_allowed = diag_col <= diag_row if chunk == 2 else diag_col > diag_row
        lane = lax.broadcasted_iota(jnp.int32, (query_block, stat_cols), 1)

        def compute():
            for block in range(blocks):
                r0 = block * query_block
                if chunk == 2:
                    pieces = [(0, r0, False), (r0, r0 + query_block, True)]
                elif chunk == 1:
                    pieces = [(0, key_rows, False)]
                else:
                    pieces = [(r0, r0 + query_block, True), (r0 + query_block, rows, False)]
                pieces = [piece for piece in pieces if piece[1] > piece[0]]
                qrows = slice(r0, r0 + query_block)
                if not first:
                    m_block = m_in[qrows, :]
                    l_block = l_in[qrows, :]
                if not last:
                    m_keep = m_out[qrows, :]
                    l_keep = l_out[qrows, :]
                for g in range(group):
                    pick = lane == group * head + g
                    cols = slice(g * HEAD_DIM, (g + 1) * HEAD_DIM)
                    query = q_ref[qrows, cols]
                    scores = []
                    for k0, k1, masked in pieces:
                        s = lax.dot_general(
                            query, k_ref[k0:k1, :], (((1,), (1,)), ((), ())),
                            preferred_element_type=jnp.float32,
                        ) * log2_scale
                        if masked:
                            s = jnp.where(diag_allowed, s, masked_score)
                        scores.append(s)
                    block_max = row_reduce(jnp.concatenate(scores, axis=1) if len(scores) > 1 else scores[0],
                                           jnp.maximum, jnp.max)
                    if first:
                        m_new = block_max
                    else:
                        m_prev = jnp.sum(jnp.where(pick, m_block, 0.0), axis=1, keepdims=True)
                        l_prev = jnp.sum(jnp.where(pick, l_block, 0.0), axis=1, keepdims=True)
                        m_new = jnp.maximum(m_prev, block_max)
                        alpha = jnp.exp2(m_prev - m_new)
                    l_part = None
                    pv = None
                    for (k0, k1, masked), s in zip(pieces, scores):
                        p = jnp.exp2(s - m_new)
                        part = row_reduce(p, jnp.add, jnp.sum)
                        l_part = part if l_part is None else l_part + part
                        term = jnp.dot(p.astype(jnp.bfloat16), v_ref[k0:k1, :],
                                       preferred_element_type=jnp.float32)
                        pv = term if pv is None else pv + term
                    if first:
                        l_new = l_part
                        acc_new = pv
                    else:
                        l_new = alpha * l_prev + l_part
                        acc_new = alpha * acc_in[qrows, cols] + pv
                    if last:
                        o_ref[qrows, cols] = (acc_new / l_new).astype(o_ref.dtype)
                    else:
                        acc_out[qrows, cols] = acc_new
                        m_keep = jnp.where(pick, m_new, m_keep)
                        l_keep = jnp.where(pick, l_new, l_keep)
                if not last:
                    m_out[qrows, :] = m_keep
                    l_out[qrows, :] = l_keep

        def passthrough():
            if last:
                all_lanes = lax.broadcasted_iota(jnp.int32, (rows, stat_cols), 1)
                l_all = l_in[...]
                for g in range(group):
                    cols = slice(g * HEAD_DIM, (g + 1) * HEAD_DIM)
                    l_prev = jnp.sum(jnp.where(all_lanes == group * head + g, l_all, 0.0),
                                     axis=1, keepdims=True)
                    o_ref[:, cols] = (acc_in[:, cols] / l_prev).astype(o_ref.dtype)
            else:
                m_out[...] = m_in[...]
                l_out[...] = l_in[...]
                acc_out[...] = acc_in[...]

        if chunk == 2:
            compute()
        else:
            valid = first_row >= (2 - chunk) * rows
            pl.when(valid)(compute)
            pl.when(jnp.logical_not(valid))(passthrough)

    return kernel


def attend_chunk(chunk, queries, pair, first_row, state):
    key_count, key_cols = pair.shape[1:]
    rows, query_cols = queries.shape
    kv_heads = key_cols // HEAD_DIM
    group = query_cols // key_cols
    heads = kv_heads * group
    first = state is None
    last = chunk == 0
    query_block = QUERY_BLOCK if chunk == 1 else MASKED_QUERY_BLOCK
    kernel = chunk_kernel(chunk, first, last, rows, key_count, query_block, group)
    q_spec = pl.BlockSpec((rows, group * HEAD_DIM), lambda h, f: (0, h))
    k_spec = pl.BlockSpec((None, key_count, HEAD_DIM), lambda h, f: (0, 0, h))
    v_spec = pl.BlockSpec((None, key_count, HEAD_DIM), lambda h, f: (1, 0, h))
    stat_spec = pl.BlockSpec((rows, heads), lambda h, f: (0, 0))
    state_specs = [stat_spec, stat_spec, q_spec]
    in_specs = [q_spec, k_spec, v_spec] + ([] if first else state_specs)
    stat_shape = jax.ShapeDtypeStruct((rows, heads), jnp.float32)
    if last:
        out_specs = q_spec
        out_shape = jax.ShapeDtypeStruct((rows, query_cols), jnp.bfloat16)
    else:
        out_specs = state_specs
        out_shape = [stat_shape, stat_shape, jax.ShapeDtypeStruct((rows, query_cols), jnp.float32)]
    keys_per_row = rows // 2 + query_block // 2 if chunk != 1 else key_count
    cost = pl.CostEstimate(
        flops=4 * heads * rows * keys_per_row * HEAD_DIM,
        transcendentals=heads * rows * keys_per_row,
        bytes_accessed=rows * query_cols * (2 + 4 + (0 if first else 4)) + 4 * key_count * key_cols,
    )
    grid_spec = pltpu.PrefetchScalarGridSpec(
        num_scalar_prefetch=1,
        grid=(kv_heads,),
        in_specs=in_specs,
        out_specs=out_specs,
    )
    return pl.pallas_call(
        kernel,
        grid_spec=grid_spec,
        out_shape=out_shape,
        cost_estimate=cost,
        compiler_params=pltpu.CompilerParams(dimension_semantics=("arbitrary",)),
    )(first_row.reshape(1), queries, pair, pair, *([] if first else state))


def swap_variant(half):
    variants = lax.axis_size("variant")
    return lax.ppermute(half, "variant", [(i, (i + 1) % variants) for i in range(variants)])


def halves_in_order(own, other, variant_index):
    return jnp.where(
        variant_index == 0,
        jnp.concatenate([own, other], axis=1),
        jnp.concatenate([other, own], axis=1),
    )


def shard_body(queries, keys, values, clean_keys, clean_values, owner_shard, span_offset, span_length):
    row_count = keys.shape[0]
    assert WINDOW == 2 * row_count
    shard_index = lax.axis_index("seq")
    first_row = (shard_index * row_count).astype(jnp.int32)
    position = lax.broadcasted_iota(jnp.int32, (row_count, span_offset.shape[1]), 0)
    in_span = (position >= span_offset) & (position < span_offset + span_length)
    in_span = in_span & (owner_shard[:, None] == shard_index)
    inside = jnp.any(in_span, axis=1)
    corrupt_pair = jnp.stack([keys, values])
    clean_own = jnp.stack([clean_keys, clean_values])
    if lax.axis_size("variant") != 2:
        clean_full = lax.all_gather(clean_own, "variant", axis=1, tiled=True)
        patched = jnp.where(inside[None, :, None], clean_full, corrupt_pair)
        near = shifted(patched, "seq", 1)
        far = shifted(near, "seq", 1)
        near_parts = (near,)
    else:
        half = row_count // 2
        variant_index = lax.axis_index("variant")
        lo, hi = corrupt_pair[:, :half], corrupt_pair[:, half:]
        inside_lo, inside_hi = inside[:half], inside[half:]
        corrupt_own = jnp.where(variant_index == 0, lo, hi)
        corrupt_other = jnp.where(variant_index == 0, hi, lo)
        inside_own = jnp.where(variant_index == 0, inside_lo, inside_hi)
        inside_other = jnp.where(variant_index == 0, inside_hi, inside_lo)
        clean_own = lax.optimization_barrier(clean_own)
        clean_other = swap_variant(clean_own)
        corrupt_other, inside_other = lax.optimization_barrier((corrupt_other, inside_other))
        own_half = jnp.where(inside_own[None, :, None], clean_own, corrupt_own)
        near_own = shifted(own_half, "seq", 1)
        other_half = jnp.where(inside_other[None, :, None], clean_other, corrupt_other)
        near_other = shifted(other_half, "seq", 1)
        far_own = shifted(near_own, "seq", 1)
        far_other = shifted(near_other, "seq", 1)
        patched = halves_in_order(own_half, other_half, variant_index)
        far = halves_in_order(far_own, far_other, variant_index)
        near_parts = (near_own, near_other)
    state = attend_chunk(2, queries, patched, first_row, None)
    for part in near_parts:
        state = attend_chunk(1, queries, part, first_row, state)
    result = attend_chunk(0, queries, far, first_row, state)
    return result[None]


def solution(mesh):
    placed = (
        P(("groups", "seq"), "mp"),
        P(("groups", "seq"), "mp"),
        P(("groups", "seq"), "mp"),
        P(("groups", "seq", "variant"), "mp"),
        P(("groups", "seq", "variant"), "mp"),
        P(("groups", "variant")),
        P(("groups", "variant"), None),
        P(("groups", "variant"), None),
    )
    return jax.shard_map(
        shard_body,
        mesh=mesh,
        in_specs=placed,
        out_specs=P("variant", ("groups", "seq"), "mp"),
        check_vma=False,
    )
```

```python
import jax
import jax.numpy as jnp
from jax import lax
from jax.experimental import pallas as pl
from jax.experimental.pallas import tpu as pltpu
from jax.sharding import PartitionSpec as P


HEAD_DIM = 128
WINDOW = 1024
QUERY_BLOCK = 512
MASKED_QUERY_BLOCK = 512

query_scale = 168.0 ** (-0.5)
log2_scale = query_scale * 1.4426950408889634
masked_score = -1e30


def shifted(shard, axis, by):
    devices = lax.axis_size(axis)
    pairs = [(i, i + by) for i in range(devices) if 0 <= i + by < devices]
    return lax.ppermute(shard, axis, pairs)


def row_reduce(x, combine, reduce):
    lanes = 128
    partial = x[:, :lanes]
    for start in range(lanes, x.shape[1], lanes):
        partial = combine(partial, x[:, start:start + lanes])
    return reduce(partial, axis=1, keepdims=True)


def chunk_kernel(chunk, first, last, rows, key_rows, query_block, group):
    blocks = rows // query_block

    def kernel(first_ref, q_ref, k_ref, v_ref, *rest):
        if first:
            m_out, l_out, acc_out = rest
        elif last:
            m_in, l_in, acc_in, o_ref = rest
        else:
            m_in, l_in, acc_in, m_out, l_out, acc_out = rest
        head = pl.program_id(0)
        first_row = first_ref[0]
        stat_cols = (m_out if first else m_in).shape[1]
        diag_shape = (query_block, query_block)
        diag_row = lax.broadcasted_iota(jnp.int32, diag_shape, 0)
        diag_col = lax.broadcasted_iota(jnp.int32, diag_shape, 1)
        diag_allowed = diag_col <= diag_row if chunk == 2 else diag_col > diag_row
        lane = lax.broadcasted_iota(jnp.int32, (query_block, stat_cols), 1)

        def compute():
            for block in range(blocks):
                r0 = block * query_block
                if chunk == 2:
                    pieces = [(0, r0, False), (r0, r0 + query_block, True)]
                elif chunk == 1:
                    pieces = [(0, key_rows, False)]
                else:
                    pieces = [(r0, r0 + query_block, True), (r0 + query_block, rows, False)]
                pieces = [piece for piece in pieces if piece[1] > piece[0]]
                qrows = slice(r0, r0 + query_block)
                if not first:
                    m_block = m_in[qrows, :]
                    l_block = l_in[qrows, :]
                if not last:
                    m_keep = m_out[qrows, :]
                    l_keep = l_out[qrows, :]
                for g in range(group):
                    pick = lane == group * head + g
                    cols = slice(g * HEAD_DIM, (g + 1) * HEAD_DIM)
                    query = q_ref[qrows, cols]
                    scores = []
                    for k0, k1, masked in pieces:
                        s = lax.dot_general(
                            query, k_ref[k0:k1, :], (((1,), (1,)), ((), ())),
                            preferred_element_type=jnp.float32,
                        ) * log2_scale
                        if masked:
                            s = jnp.where(diag_allowed, s, masked_score)
                        scores.append(s)
                    block_max = row_reduce(jnp.concatenate(scores, axis=1) if len(scores) > 1 else scores[0],
                                           jnp.maximum, jnp.max)
                    if first:
                        m_new = block_max
                    else:
                        m_prev = jnp.sum(jnp.where(pick, m_block, 0.0), axis=1, keepdims=True)
                        l_prev = jnp.sum(jnp.where(pick, l_block, 0.0), axis=1, keepdims=True)
                        m_new = jnp.maximum(m_prev, block_max)
                        alpha = jnp.exp2(m_prev - m_new)
                    l_part = None
                    pv = None
                    for (k0, k1, masked), s in zip(pieces, scores):
                        p = jnp.exp2(s - m_new)
                        part = row_reduce(p, jnp.add, jnp.sum)
                        l_part = part if l_part is None else l_part + part
                        term = jnp.dot(p.astype(jnp.bfloat16), v_ref[k0:k1, :],
                                       preferred_element_type=jnp.float32)
                        pv = term if pv is None else pv + term
                    if first:
                        l_new = l_part
                        acc_new = pv
                    else:
                        l_new = alpha * l_prev + l_part
                        acc_new = alpha * acc_in[qrows, cols] + pv
                    if last:
                        o_ref[qrows, cols] = (acc_new / l_new).astype(o_ref.dtype)
                    else:
                        acc_out[qrows, cols] = acc_new
                        m_keep = jnp.where(pick, m_new, m_keep)
                        l_keep = jnp.where(pick, l_new, l_keep)
                if not last:
                    m_out[qrows, :] = m_keep
                    l_out[qrows, :] = l_keep

        def passthrough():
            if last:
                all_lanes = lax.broadcasted_iota(jnp.int32, (rows, stat_cols), 1)
                l_all = l_in[...]
                for g in range(group):
                    cols = slice(g * HEAD_DIM, (g + 1) * HEAD_DIM)
                    l_prev = jnp.sum(jnp.where(all_lanes == group * head + g, l_all, 0.0),
                                     axis=1, keepdims=True)
                    o_ref[:, cols] = (acc_in[:, cols] / l_prev).astype(o_ref.dtype)
            else:
                m_out[...] = m_in[...]
                l_out[...] = l_in[...]
                acc_out[...] = acc_in[...]

        if chunk == 2:
            compute()
        else:
            valid = first_row >= (2 - chunk) * rows
            pl.when(valid)(compute)
            pl.when(jnp.logical_not(valid))(passthrough)

    return kernel


def attend_chunk(chunk, queries, pair, first_row, state):
    key_count, key_cols = pair.shape[1:]
    rows, query_cols = queries.shape
    kv_heads = key_cols // HEAD_DIM
    group = query_cols // key_cols
    heads = kv_heads * group
    first = state is None
    last = chunk == 0
    query_block = QUERY_BLOCK if chunk == 1 else MASKED_QUERY_BLOCK
    kernel = chunk_kernel(chunk, first, last, rows, key_count, query_block, group)
    q_spec = pl.BlockSpec((rows, group * HEAD_DIM), lambda h, f: (0, h))
    k_spec = pl.BlockSpec((None, key_count, HEAD_DIM), lambda h, f: (0, 0, h))
    v_spec = pl.BlockSpec((None, key_count, HEAD_DIM), lambda h, f: (1, 0, h))
    stat_spec = pl.BlockSpec((rows, heads), lambda h, f: (0, 0))
    state_specs = [stat_spec, stat_spec, q_spec]
    in_specs = [q_spec, k_spec, v_spec] + ([] if first else state_specs)
    stat_shape = jax.ShapeDtypeStruct((rows, heads), jnp.float32)
    if last:
        out_specs = q_spec
        out_shape = jax.ShapeDtypeStruct((rows, query_cols), jnp.bfloat16)
    else:
        out_specs = state_specs
        out_shape = [stat_shape, stat_shape, jax.ShapeDtypeStruct((rows, query_cols), jnp.float32)]
    keys_per_row = rows // 2 + query_block // 2 if chunk != 1 else key_count
    cost = pl.CostEstimate(
        flops=4 * heads * rows * keys_per_row * HEAD_DIM,
        transcendentals=heads * rows * keys_per_row,
        bytes_accessed=rows * query_cols * (2 + 4 + (0 if first else 4)) + 4 * key_count * key_cols,
    )
    grid_spec = pltpu.PrefetchScalarGridSpec(
        num_scalar_prefetch=1,
        grid=(kv_heads,),
        in_specs=in_specs,
        out_specs=out_specs,
    )
    return pl.pallas_call(
        kernel,
        grid_spec=grid_spec,
        out_shape=out_shape,
        cost_estimate=cost,
        compiler_params=pltpu.CompilerParams(dimension_semantics=("arbitrary",)),
    )(first_row.reshape(1), queries, pair, pair, *([] if first else state))


def swap_variant(half):
    variants = lax.axis_size("variant")
    return lax.ppermute(half, "variant", [(i, (i + 1) % variants) for i in range(variants)])


def halves_in_order(own, other, variant_index):
    return jnp.where(
        variant_index == 0,
        jnp.concatenate([own, other], axis=1),
        jnp.concatenate([other, own], axis=1),
    )


def shard_body(queries, keys, values, clean_keys, clean_values, owner_shard, span_offset, span_length):
    row_count = keys.shape[0]
    assert WINDOW == 2 * row_count
    shard_index = lax.axis_index("seq")
    first_row = (shard_index * row_count).astype(jnp.int32)
    position = lax.broadcasted_iota(jnp.int32, (row_count, span_offset.shape[1]), 0)
    in_span = (position >= span_offset) & (position < span_offset + span_length)
    in_span = in_span & (owner_shard[:, None] == shard_index)
    inside = jnp.any(in_span, axis=1)
    corrupt_pair = jnp.stack([keys, values])
    clean_own = jnp.stack([clean_keys, clean_values])
    if lax.axis_size("variant") != 2:
        clean_full = lax.all_gather(clean_own, "variant", axis=1, tiled=True)
        patched = jnp.where(inside[None, :, None], clean_full, corrupt_pair)
        near = shifted(patched, "seq", 1)
        far = shifted(near, "seq", 1)
        near_parts = (near,)
    else:
        half = row_count // 2
        variant_index = lax.axis_index("variant")
        lo, hi = corrupt_pair[:, :half], corrupt_pair[:, half:]
        inside_lo, inside_hi = inside[:half], inside[half:]
        corrupt_own = jnp.where(variant_index == 0, lo, hi)
        corrupt_other = jnp.where(variant_index == 0, hi, lo)
        inside_own = jnp.where(variant_index == 0, inside_lo, inside_hi)
        inside_other = jnp.where(variant_index == 0, inside_hi, inside_lo)
        clean_own = lax.optimization_barrier(clean_own)
        clean_other = swap_variant(clean_own)
        corrupt_other, inside_other = lax.optimization_barrier((corrupt_other, inside_other))
        own_half = jnp.where(inside_own[None, :, None], clean_own, corrupt_own)
        near_own = shifted(own_half, "seq", 1)
        other_half = jnp.where(inside_other[None, :, None], clean_other, corrupt_other)
        near_other = shifted(other_half, "seq", 1)
        far_own = shifted(near_own, "seq", 1)
        far_other = shifted(near_other, "seq", 1)
        patched = halves_in_order(own_half, other_half, variant_index)
        far_placed = lax.dynamic_update_slice_in_dim(
            jnp.zeros(far_own.shape[:1] + (row_count,) + far_own.shape[2:], far_own.dtype),
            far_own, half * variant_index, 1)
        far = lax.dynamic_update_slice_in_dim(far_placed, far_other, half * (1 - variant_index), 1)
        near_parts = (near_own, near_other)
    state = attend_chunk(2, queries, patched, first_row, None)
    for part in near_parts:
        state = attend_chunk(1, queries, part, first_row, state)
    result = attend_chunk(0, queries, far, first_row, state)
    return result[None]


def solution(mesh):
    placed = (
        P(("groups", "seq"), "mp"),
        P(("groups", "seq"), "mp"),
        P(("groups", "seq"), "mp"),
        P(("groups", "seq", "variant"), "mp"),
        P(("groups", "seq", "variant"), "mp"),
        P(("groups", "variant")),
        P(("groups", "variant"), None),
        P(("groups", "variant"), None),
    )
    return jax.shard_map(
        shard_body,
        mesh=mesh,
        in_specs=placed,
        out_specs=P("variant", ("groups", "seq"), "mp"),
        check_vma=False,
    )
```

```python
import jax
import jax.numpy as jnp
from jax import lax
from jax.experimental import pallas as pl
from jax.experimental.pallas import tpu as pltpu
from jax.sharding import PartitionSpec as P


HEAD_DIM = 128
WINDOW = 1024
QUERY_BLOCK = 512
MASKED_QUERY_BLOCK = 512

query_scale = 168.0 ** (-0.5)
log2_scale = query_scale * 1.4426950408889634
masked_score = -1e30


def shifted(shard, axis, by):
    devices = lax.axis_size(axis)
    pairs = [(i, i + by) for i in range(devices) if 0 <= i + by < devices]
    return lax.ppermute(shard, axis, pairs)


def row_reduce(x, combine, reduce):
    lanes = 128
    partial = x[:, :lanes]
    for start in range(lanes, x.shape[1], lanes):
        partial = combine(partial, x[:, start:start + lanes])
    return reduce(partial, axis=1, keepdims=True)


def chunk_kernel(chunk, first, last, rows, key_rows, query_block, group):
    blocks = rows // query_block

    def kernel(first_ref, q_ref, k_ref, v_ref, *rest):
        if first:
            m_out, l_out, acc_out = rest
        elif last:
            m_in, l_in, acc_in, o_ref = rest
        else:
            m_in, l_in, acc_in, m_out, l_out, acc_out = rest
        head = pl.program_id(0)
        first_row = first_ref[0]
        stat_cols = (m_out if first else m_in).shape[1]
        diag_shape = (query_block, query_block)
        diag_row = lax.broadcasted_iota(jnp.int32, diag_shape, 0)
        diag_col = lax.broadcasted_iota(jnp.int32, diag_shape, 1)
        diag_allowed = diag_col <= diag_row if chunk == 2 else diag_col > diag_row
        lane = lax.broadcasted_iota(jnp.int32, (query_block, stat_cols), 1)

        def compute():
            for block in range(blocks):
                r0 = block * query_block
                if chunk == 2:
                    pieces = [(0, r0, False), (r0, r0 + query_block, True)]
                elif chunk == 1:
                    pieces = [(0, key_rows, False)]
                else:
                    pieces = [(r0, r0 + query_block, True), (r0 + query_block, rows, False)]
                pieces = [piece for piece in pieces if piece[1] > piece[0]]
                qrows = slice(r0, r0 + query_block)
                if not first:
                    m_block = m_in[qrows, :]
                    l_block = l_in[qrows, :]
                if not last:
                    m_keep = m_out[qrows, :]
                    l_keep = l_out[qrows, :]
                for g in range(group):
                    pick = lane == group * head + g
                    cols = slice(g * HEAD_DIM, (g + 1) * HEAD_DIM)
                    query = q_ref[qrows, cols]
                    scores = []
                    for k0, k1, masked in pieces:
                        s = lax.dot_general(
                            query, k_ref[k0:k1, :], (((1,), (1,)), ((), ())),
                            preferred_element_type=jnp.float32,
                        ) * log2_scale
                        if masked:
                            s = jnp.where(diag_allowed, s, masked_score)
                        scores.append(s)
                    block_max = row_reduce(jnp.concatenate(scores, axis=1) if len(scores) > 1 else scores[0],
                                           jnp.maximum, jnp.max)
                    if first:
                        m_new = block_max
                    else:
                        m_prev = jnp.sum(jnp.where(pick, m_block, 0.0), axis=1, keepdims=True)
                        l_prev = jnp.sum(jnp.where(pick, l_block, 0.0), axis=1, keepdims=True)
                        m_new = jnp.maximum(m_prev, block_max)
                        alpha = jnp.exp2(m_prev - m_new)
                    l_part = None
                    pv = None
                    for (k0, k1, masked), s in zip(pieces, scores):
                        p = jnp.exp2(s - m_new)
                        part = row_reduce(p, jnp.add, jnp.sum)
                        l_part = part if l_part is None else l_part + part
                        term = jnp.dot(p.astype(jnp.bfloat16), v_ref[k0:k1, :],
                                       preferred_element_type=jnp.float32)
                        pv = term if pv is None else pv + term
                    if first:
                        l_new = l_part
                        acc_new = pv
                    else:
                        l_new = alpha * l_prev + l_part
                        acc_new = alpha * acc_in[qrows, cols] + pv
                    if last:
                        o_ref[qrows, cols] = (acc_new / l_new).astype(o_ref.dtype)
                    else:
                        acc_out[qrows, cols] = acc_new
                        m_keep = jnp.where(pick, m_new, m_keep)
                        l_keep = jnp.where(pick, l_new, l_keep)
                if not last:
                    m_out[qrows, :] = m_keep
                    l_out[qrows, :] = l_keep

        def passthrough():
            if last:
                all_lanes = lax.broadcasted_iota(jnp.int32, (rows, stat_cols), 1)
                l_all = l_in[...]
                for g in range(group):
                    cols = slice(g * HEAD_DIM, (g + 1) * HEAD_DIM)
                    l_prev = jnp.sum(jnp.where(all_lanes == group * head + g, l_all, 0.0),
                                     axis=1, keepdims=True)
                    o_ref[:, cols] = (acc_in[:, cols] / l_prev).astype(o_ref.dtype)
            else:
                m_out[...] = m_in[...]
                l_out[...] = l_in[...]
                acc_out[...] = acc_in[...]

        if chunk == 2:
            compute()
        else:
            valid = first_row >= (2 - chunk) * rows
            pl.when(valid)(compute)
            pl.when(jnp.logical_not(valid))(passthrough)

    return kernel


def attend_chunk(chunk, queries, pair, first_row, state):
    key_count, key_cols = pair.shape[1:]
    rows, query_cols = queries.shape
    kv_heads = key_cols // HEAD_DIM
    group = query_cols // key_cols
    heads = kv_heads * group
    first = state is None
    last = chunk == 0
    query_block = QUERY_BLOCK if chunk == 1 else MASKED_QUERY_BLOCK
    kernel = chunk_kernel(chunk, first, last, rows, key_count, query_block, group)
    q_spec = pl.BlockSpec((rows, group * HEAD_DIM), lambda h, f: (0, h))
    k_spec = pl.BlockSpec((None, key_count, HEAD_DIM), lambda h, f: (0, 0, h))
    v_spec = pl.BlockSpec((None, key_count, HEAD_DIM), lambda h, f: (1, 0, h))
    stat_spec = pl.BlockSpec((rows, heads), lambda h, f: (0, 0))
    state_specs = [stat_spec, stat_spec, q_spec]
    in_specs = [q_spec, k_spec, v_spec] + ([] if first else state_specs)
    stat_shape = jax.ShapeDtypeStruct((rows, heads), jnp.float32)
    if last:
        out_specs = q_spec
        out_shape = jax.ShapeDtypeStruct((rows, query_cols), jnp.bfloat16)
    else:
        out_specs = state_specs
        out_shape = [stat_shape, stat_shape, jax.ShapeDtypeStruct((rows, query_cols), jnp.float32)]
    keys_per_row = rows // 2 + query_block // 2 if chunk != 1 else key_count
    cost = pl.CostEstimate(
        flops=4 * heads * rows * keys_per_row * HEAD_DIM,
        transcendentals=heads * rows * keys_per_row,
        bytes_accessed=rows * query_cols * (2 + 4 + (0 if first else 4)) + 4 * key_count * key_cols,
    )
    grid_spec = pltpu.PrefetchScalarGridSpec(
        num_scalar_prefetch=1,
        grid=(kv_heads,),
        in_specs=in_specs,
        out_specs=out_specs,
    )
    return pl.pallas_call(
        kernel,
        grid_spec=grid_spec,
        out_shape=out_shape,
        cost_estimate=cost,
        compiler_params=pltpu.CompilerParams(dimension_semantics=("arbitrary",)),
    )(first_row.reshape(1), queries, pair, pair, *([] if first else state))


def swap_variant(half):
    variants = lax.axis_size("variant")
    return lax.ppermute(half, "variant", [(i, (i + 1) % variants) for i in range(variants)])


def halves_in_order(own, other, variant_index):
    return jnp.where(
        variant_index == 0,
        jnp.concatenate([own, other], axis=1),
        jnp.concatenate([other, own], axis=1),
    )


def shard_body(queries, keys, values, clean_keys, clean_values, owner_shard, span_offset, span_length):
    row_count = keys.shape[0]
    assert WINDOW == 2 * row_count
    shard_index = lax.axis_index("seq")
    first_row = (shard_index * row_count).astype(jnp.int32)
    position = lax.broadcasted_iota(jnp.int32, (row_count, span_offset.shape[1]), 0)
    in_span = (position >= span_offset) & (position < span_offset + span_length)
    in_span = in_span & (owner_shard[:, None] == shard_index)
    inside = jnp.any(in_span, axis=1)
    corrupt_pair = jnp.stack([keys, values])
    clean_own = jnp.stack([clean_keys, clean_values])
    if lax.axis_size("variant") != 2:
        clean_full = lax.all_gather(clean_own, "variant", axis=1, tiled=True)
        patched = jnp.where(inside[None, :, None], clean_full, corrupt_pair)
        near = shifted(patched, "seq", 1)
        far = shifted(near, "seq", 1)
        near_parts = (near,)
    else:
        half = row_count // 2
        variant_index = lax.axis_index("variant")
        lo, hi = corrupt_pair[:, :half], corrupt_pair[:, half:]
        inside_lo, inside_hi = inside[:half], inside[half:]
        corrupt_own = jnp.where(variant_index == 0, lo, hi)
        corrupt_other = jnp.where(variant_index == 0, hi, lo)
        inside_own = jnp.where(variant_index == 0, inside_lo, inside_hi)
        inside_other = jnp.where(variant_index == 0, inside_hi, inside_lo)
        clean_k, clean_v = lax.optimization_barrier((clean_keys, clean_values))
        other_k, other_v = swap_variant((clean_k, clean_v))
        clean_other = jnp.stack([other_k, other_v])
        clean_own = jnp.stack([clean_k, clean_v])
        corrupt_other, inside_other = lax.optimization_barrier((corrupt_other, inside_other))
        own_half = jnp.where(inside_own[None, :, None], clean_own, corrupt_own)
        near_own = shifted(own_half, "seq", 1)
        other_half = jnp.where(inside_other[None, :, None], clean_other, corrupt_other)
        near_other = shifted(other_half, "seq", 1)
        far_own = shifted(near_own, "seq", 1)
        far_other = shifted(near_other, "seq", 1)
        patched = halves_in_order(own_half, other_half, variant_index)
        far_placed = lax.dynamic_update_slice_in_dim(
            jnp.zeros(far_own.shape[:1] + (row_count,) + far_own.shape[2:], far_own.dtype),
            far_own, half * variant_index, 1)
        far = lax.dynamic_update_slice_in_dim(far_placed, far_other, half * (1 - variant_index), 1)
        near_parts = (near_own, near_other)
    state = attend_chunk(2, queries, patched, first_row, None)
    for part in near_parts:
        state = attend_chunk(1, queries, part, first_row, state)
    result = attend_chunk(0, queries, far, first_row, state)
    return result[None]


def solution(mesh):
    placed = (
        P(("groups", "seq"), "mp"),
        P(("groups", "seq"), "mp"),
        P(("groups", "seq"), "mp"),
        P(("groups", "seq", "variant"), "mp"),
        P(("groups", "seq", "variant"), "mp"),
        P(("groups", "variant")),
        P(("groups", "variant"), None),
        P(("groups", "variant"), None),
    )
    return jax.shard_map(
        shard_body,
        mesh=mesh,
        in_specs=placed,
        out_specs=P("variant", ("groups", "seq"), "mp"),
        check_vma=False,
    )
```
